512 devices in a mesh: section: 16 (over y, core), seq: 32 (over x, z).
Axes of the slice: x: 4, y: 8, z: 8, core: 2. Of those that a mesh axis runs over, the one named last changes fastest.
Arguments:
- queries: bfloat16 [16, 4096, 4096], P('section', 'seq'), may hold values from -15 to 15, as said below
- keys: bfloat16 [16, 4096, 512], P('section', 'seq'), may hold values from -6 to 6, as said below
- values: bfloat16 [16, 4096, 512], P('section', 'seq'), may hold values from -6 to 6
- cache_keys: bfloat16 [16, 32, 512, 128], P('section', 'seq'), may hold values from -6 to 6
- cache_values: bfloat16 [16, 32, 512, 128], P('section', 'seq'), may hold values from -6 to 6
- vertical: int32 [16, 32, 32], P('section', 'seq'), may hold values from 0 to 63, as said below
- vertical_count: int32 [16, 32], P('section', 'seq'), may hold values from 1 to 32, as said below
- slash: int32 [16, 32, 11], P('section', 'seq'), may hold values from 1 to 127, as said below
Outputs:
- attended: bfloat16 [16, 4096, 4096], P('section', 'seq')
The draws below stay inside these ranges and needn't reach their ends.
Inputs may be any that keep to these rules, and one draw needn't show every extreme that they name: queries within the range in both draws. keys within the range in both draws. `vertical`: for each layer and head, the 32 entries are distinct cached block indices. `vertical_count`: in every layer some head uses all 32 slots. `slash`: for each layer and head, the 11 offsets are distinct.
All inputs are finite; a program needn't handle non-finite values.
Results may differ from the reference program's by a relative error of at most 0.011.
Values may be sent and summed in bfloat16 or wider, within the bound.
No kernel may reach another device: no remote copies, remote signals or barrier semaphores. Data moves between devices by JAX's collectives and lax.ppermute only.
A program may use at most 64 MiB of HBM per device.

```python
import math
import jax
import jax.numpy as jnp
from jax import lax

HEAD_SIZE = 128
GROUP = 8
BLK = 64
NVMAX = 32
NS = 11
CACHE = 4096
STRETCH = 4096
HQ = 32
KVH = 4
LAYERS = 16


def draw_queries(key, part):
    own_key = jax.random.fold_in(key, 1)
    base = jnp.clip(2.5 * jax.random.normal(own_key, (LAYERS, STRETCH, HQ * HEAD_SIZE)), -15.0, 15.0)
    return base.astype(jnp.bfloat16)


def draw_keys(key, part):
    own_key = jax.random.fold_in(key, 2)
    base = jnp.clip(jax.random.normal(own_key, (LAYERS, STRETCH, KVH * HEAD_SIZE)), -6.0, 6.0)
    return base.astype(jnp.bfloat16)


def draw_vertical(key, part):
    streams = jax.random.split(jax.random.fold_in(key, 3), LAYERS * HQ)
    picks = jax.vmap(lambda single: jax.random.permutation(single, CACHE // BLK)[:NVMAX])(streams)
    return picks.reshape(LAYERS, HQ, NVMAX).astype(jnp.int32)


def draw_vertical_count(key, part):
    spread = jax.random.randint(jax.random.fold_in(key, 4), (LAYERS, HQ), 0, 17)
    count = 1 + spread * spread * (NVMAX - 1) // 256
    heavy = jax.random.randint(jax.random.fold_in(key, 5), (LAYERS, 1), 0, HQ)
    count = jnp.where(jnp.arange(HQ)[None, :] == heavy, NVMAX, count)
    return count.astype(jnp.int32)


def draw_slash(key, part):
    streams = jax.random.split(jax.random.fold_in(key, 6), LAYERS * HQ)
    picks = jax.vmap(lambda single: jax.random.permutation(single, CACHE // BLK + STRETCH // BLK - 1)[:NS])(streams)
    return (picks + 1).reshape(LAYERS, HQ, NS).astype(jnp.int32)


def block_scale(key, dims, cuts, smallest, largest):
    gain, own = 1.0, jax.random.fold_in(key, 6)
    for axis_at, blocks in cuts:
        steps = jnp.exp(jax.random.uniform(jax.random.fold_in(own, axis_at), (blocks,), jnp.float32, smallest / len(cuts), largest / len(cuts)))
        gain = gain * jnp.repeat(steps, dims[axis_at] // blocks).reshape([-1 if axis == axis_at else 1 for axis in range(len(dims))])
    return gain


def noise(key, extent, scale, limit, pieces=(), held_as=jnp.bfloat16):
    result = scale * jax.random.normal(key, extent, jnp.float32)
    if pieces:
        result = result * block_scale(key, extent, pieces, -0.22, 0.18)
    return jnp.clip(result, -limit, limit).astype(held_as)


def setup_inputs(seed: int = 0) -> dict:
    streams_of = jax.random.split(jax.random.key(seed), 9)
    queries = draw_queries(jax.random.fold_in(streams_of[8], 71), 0)
    keys = draw_keys(jax.random.fold_in(streams_of[8], 71), 0)
    values = noise(streams_of[2], (LAYERS, STRETCH, KVH * HEAD_SIZE), 1.0, 6.0, ((0, 16), (1, 32)))
    cache_keys = noise(streams_of[3], (LAYERS, KVH * GROUP, CACHE // GROUP, HEAD_SIZE), 1.0, 6.0, ((0, 16), (1, 32)))
    cache_values = noise(streams_of[4], (LAYERS, KVH * GROUP, CACHE // GROUP, HEAD_SIZE), 1.0, 6.0, ((0, 16), (1, 32)))
    vertical = draw_vertical(jax.random.fold_in(streams_of[8], 71), 0)
    vertical_count = draw_vertical_count(jax.random.fold_in(streams_of[8], 71), 0)
    slash = draw_slash(jax.random.fold_in(streams_of[8], 71), 0)
    return {"queries": queries, "keys": keys, "values": values, "cache_keys": cache_keys, "cache_values": cache_values, "vertical": vertical, "vertical_count": vertical_count, "slash": slash}


big_negative = -1e+30

def head_attention(query_matrix, gathered_keys, gathered_values, verts, count, slashes):
    prefill_stretch = query_matrix.shape[0]
    ncb = CACHE // BLK
    nqb = prefill_stretch // BLK
    softmax_scale = 1.0 / math.sqrt(HEAD_SIZE)
    inner = jnp.arange(BLK, dtype=jnp.int32)
    vertical_row_index = (verts[:, None].astype(jnp.int32) * BLK + inner[None, :]).reshape(-1)
    vertical_key_rows = jnp.take(gathered_keys, vertical_row_index, axis=0)
    vertical_value_rows = jnp.take(gathered_values, vertical_row_index, axis=0)
    vlive = jnp.repeat(jnp.arange(NVMAX, dtype=jnp.int32) < count, BLK)
    vertical_block_list = jnp.dot(query_matrix, vertical_key_rows.T, preferred_element_type=jnp.float32) * softmax_scale
    offsets = jnp.concatenate([jnp.zeros((1,), jnp.int32), slashes.astype(jnp.int32)])
    blocks = ncb + jnp.arange(nqb, dtype=jnp.int32)[:, None] - offsets[None, :]
    used = jnp.arange(NVMAX, dtype=jnp.int32)[None, None, :] < count
    listed = jnp.any((blocks[:, :, None] == verts[None, None, :].astype(jnp.int32)) & used, axis=2)
    valid = (blocks >= 0) & jnp.logical_not(listed)
    safe = jnp.maximum(blocks, 0)
    width = (NS + 1) * BLK
    slash_row_index = (safe[:, :, None] * BLK + inner[None, None, :]).reshape(nqb, width)
    slash_key_rows = jnp.take(gathered_keys, slash_row_index, axis=0)
    slash_value_rows = jnp.take(gathered_values, slash_row_index, axis=0)
    query_block_count = query_matrix.reshape(nqb, BLK, HEAD_SIZE)
    slash_block_list = jnp.einsum('cra,cma->crm', query_block_count.astype(jnp.float32), slash_key_rows.astype(jnp.float32)) * softmax_scale
    column = jnp.arange(width, dtype=jnp.int32)
    causal = (column[None, :] >= BLK) | ((column % BLK)[None, :] <= inner[:, None])
    smask = jnp.repeat(valid, BLK, axis=1)[:, None, :] & causal[None, :, :]
    vtop = lax.optimization_barrier(jnp.max(jnp.where(vlive[None, :], vertical_block_list, big_negative), axis=1))
    stop = lax.optimization_barrier(jnp.max(jnp.where(smask, slash_block_list, big_negative), axis=2)).reshape(prefill_stretch)
    top = jnp.maximum(vtop, stop)
    vertical_probabilities = jnp.where(vlive[None, :], jnp.exp(vertical_block_list - top[:, None]), 0.0)
    slash_probabilities = jnp.where(smask, jnp.exp(slash_block_list - top.reshape(nqb, BLK, 1)), 0.0)
    total = lax.optimization_barrier(jnp.sum(vertical_probabilities, axis=1)) + lax.optimization_barrier(jnp.sum(slash_probabilities, axis=2)).reshape(prefill_stretch)
    output_running = jnp.dot(vertical_probabilities.astype(jnp.bfloat16), vertical_value_rows, preferred_element_type=jnp.float32)
    output_running = output_running + jnp.einsum('owu,out->owt', slash_probabilities.astype(jnp.bfloat16).astype(jnp.float32), slash_value_rows.astype(jnp.float32)).reshape(prefill_stretch, HEAD_SIZE)
    return (output_running / total[:, None]).astype(jnp.bfloat16)

def reference(queries, keys, values, cache_keys, cache_values, vertical, vertical_count, slash):
    q_in = jnp.roll(queries, 1, axis=0)
    k_in = jnp.roll(keys, 1, axis=0)
    v_in = jnp.roll(values, 1, axis=0)
    layers = queries.shape[0]
    prefill_stretch = queries.shape[1]
    heads = vertical.shape[1]

    def one(index):
        layer = index // heads
        head = index % heads
        group_id = head // GROUP
        query_matrix = lax.dynamic_slice_in_dim(lax.dynamic_index_in_dim(q_in, layer, 0, keepdims=False), head * HEAD_SIZE, HEAD_SIZE, axis=1)
        stretch_keys = lax.dynamic_slice_in_dim(lax.dynamic_index_in_dim(k_in, layer, 0, keepdims=False), group_id * HEAD_SIZE, HEAD_SIZE, axis=1)
        stretch_vals = lax.dynamic_slice_in_dim(lax.dynamic_index_in_dim(v_in, layer, 0, keepdims=False), group_id * HEAD_SIZE, HEAD_SIZE, axis=1)
        old_keys = lax.dynamic_slice_in_dim(lax.dynamic_index_in_dim(cache_keys, layer, 0, keepdims=False), group_id * GROUP, GROUP, axis=0).reshape(CACHE, HEAD_SIZE)
        old_vals = lax.dynamic_slice_in_dim(lax.dynamic_index_in_dim(cache_values, layer, 0, keepdims=False), group_id * GROUP, GROUP, axis=0).reshape(CACHE, HEAD_SIZE)
        gathered_keys = jnp.concatenate([old_keys, stretch_keys], axis=0)
        gathered_values = jnp.concatenate([old_vals, stretch_vals], axis=0)
        verts = vertical[layer, head]
        count = vertical_count[layer, head]
        slashes = slash[layer, head]
        return head_attention(query_matrix, gathered_keys, gathered_values, verts, count, slashes)
    outcome = lax.map(one, jnp.arange(layers * heads, dtype=jnp.int32))
    outcome = outcome.reshape(layers, heads, prefill_stretch, HEAD_SIZE).transpose(0, 2, 1, 3)
    return outcome.reshape(layers, prefill_stretch, heads * HEAD_SIZE)
```

```python
import math

import jax
import jax.numpy as jnp
from jax import lax
from jax.experimental import pallas as pl
from jax.experimental.pallas import tpu as pltpu
from jax.sharding import Mesh
from jax.sharding import PartitionSpec as P

HEAD_SIZE = 128
GROUP = 8
BLK = 64
NVMAX = 32
NS = 11
CACHE = 4096
TQ = 256

big_negative = -1e30


def from_behind(x, axis, by):
    peers = lax.axis_size(axis)
    return lax.ppermute(x, axis, [(i, (i + by) % peers) for i in range(peers)])


def attention_kernel(verts_ref, count_ref, sblk_ref, q_ref, k_ref, v_ref, smask_ref, o_ref,
                     kvert, vvert, kslash, vslash):
    nb = TQ // BLK
    nd = NS + 1
    width = nd * BLK
    nvc = NVMAX * BLK
    tile = pl.program_id(0)
    softmax_scale = 1.0 / math.sqrt(HEAD_SIZE)
    ncb = CACHE // BLK

    @pl.when(tile == 0)
    def _():
        def fill(s, carry):
            blk = jnp.clip(verts_ref[s], 0, ncb - 1)
            src = pl.multiple_of(blk * BLK, BLK)
            dst = pl.multiple_of(s * BLK, BLK)
            kvert[pl.ds(dst, BLK), :] = k_ref[pl.ds(src, BLK), :]
            vvert[pl.ds(dst, BLK), :] = v_ref[pl.ds(src, BLK), :]
            return carry

        lax.fori_loop(0, NVMAX, fill, 0)

    for b in range(nb):
        qb = tile * nb + b
        for d in range(nd):
            blk = sblk_ref[qb * nd + d]
            src = pl.multiple_of(blk * BLK, BLK)
            kslash[b, pl.ds(d * BLK, BLK), :] = k_ref[pl.ds(src, BLK), :]
            vslash[b, pl.ds(d * BLK, BLK), :] = v_ref[pl.ds(src, BLK), :]

    q = q_ref[...]
    count = count_ref[0]
    s_v = lax.dot_general(q, kvert[...], (((1,), (1,)), ((), ())),
                          preferred_element_type=jnp.float32) * softmax_scale
    vcol = lax.broadcasted_iota(jnp.int32, (1, nvc), 1)
    vlive = vcol < count * BLK
    s_v = jnp.where(vlive, s_v, big_negative)
    q3 = q.reshape(nb, BLK, HEAD_SIZE)
    s_s = lax.dot_general(q3, kslash[...], (((2,), (2,)), ((0,), (0,))),
                          preferred_element_type=jnp.float32) * softmax_scale
    col = lax.broadcasted_iota(jnp.int32, (nb, BLK, width), 2)
    row = lax.broadcasted_iota(jnp.int32, (nb, BLK, width), 1)
    causal = (col >= BLK) | (col <= row)
    smask = (smask_ref[...] > 0) & causal
    s_s = jnp.where(smask, s_s, big_negative)
    top_v = jnp.max(s_v, axis=1, keepdims=True).reshape(nb, BLK, 1)
    top_s = jnp.max(s_s, axis=2, keepdims=True)
    top = jnp.maximum(top_v, top_s)
    p_v = jnp.where(vlive, jnp.exp(s_v - top.reshape(TQ, 1)), 0.0)
    p_s = jnp.where(smask, jnp.exp(s_s - top), 0.0)
    total = jnp.sum(p_v, axis=1, keepdims=True).reshape(nb, BLK, 1) + jnp.sum(
        p_s, axis=2, keepdims=True)
    acc_v = jnp.dot(p_v.astype(jnp.bfloat16), vvert[...], preferred_element_type=jnp.float32)
    acc_s = lax.dot_general(p_s.astype(jnp.bfloat16), vslash[...], (((2,), (1,)), ((0,), (0,))),
                            preferred_element_type=jnp.float32)
    acc = acc_v.reshape(nb, BLK, HEAD_SIZE) + acc_s
    o_ref[...] = (acc / total).reshape(TQ, HEAD_SIZE).astype(o_ref.dtype)


def head_attention(own_query, all_k, all_v, verts, count, slashes):
    prefill_stretch = own_query.shape[0]
    ncb = CACHE // BLK
    nqb = prefill_stretch // BLK
    nd = NS + 1
    offsets = jnp.concatenate([jnp.zeros((1,), jnp.int32), slashes])
    blocks = ncb + jnp.arange(nqb, dtype=jnp.int32)[:, None] - offsets[None, :]
    used = jnp.arange(NVMAX, dtype=jnp.int32)[None, None, :] < count
    listed = jnp.any((blocks[:, :, None] == verts[None, None, :]) & used, axis=2)
    valid = (blocks >= 0) & jnp.logical_not(listed)
    sblk = jnp.clip(blocks, 0, all_k.shape[0] // BLK - 1).reshape(-1)
    smask = jnp.repeat(valid.astype(jnp.int32), BLK, axis=1).reshape(nqb, 1, nd * BLK)
    nb = TQ // BLK
    grid_spec = pltpu.PrefetchScalarGridSpec(
        num_scalar_prefetch=3,
        grid=(prefill_stretch // TQ,),
        in_specs=[
            pl.BlockSpec((TQ, HEAD_SIZE), lambda i, *_: (i, 0)),
            pl.BlockSpec(all_k.shape, lambda i, *_: (0, 0)),
            pl.BlockSpec(all_v.shape, lambda i, *_: (0, 0)),
            pl.BlockSpec((nb, 1, nd * BLK), lambda i, *_: (i, 0, 0)),
        ],
        out_specs=pl.BlockSpec((TQ, HEAD_SIZE), lambda i, *_: (i, 0)),
        scratch_shapes=[
            pltpu.VMEM((NVMAX * BLK, HEAD_SIZE), jnp.bfloat16),
            pltpu.VMEM((NVMAX * BLK, HEAD_SIZE), jnp.bfloat16),
            pltpu.VMEM((nb, nd * BLK, HEAD_SIZE), jnp.bfloat16),
            pltpu.VMEM((nb, nd * BLK, HEAD_SIZE), jnp.bfloat16),
        ],
    )
    return pl.pallas_call(
        attention_kernel,
        grid_spec=grid_spec,
        out_shape=jax.ShapeDtypeStruct((prefill_stretch, HEAD_SIZE), jnp.bfloat16),
        compiler_params=pltpu.CompilerParams(dimension_semantics=("arbitrary",)),
    )(verts, count.reshape(1), sblk, own_query, all_k, all_v, smask)


def per_device(queries, keys, values, cache_keys, cache_values, vertical, vertical_count, slash):
    query_rows, key_rows, value_rows = from_behind((queries, keys, values), "section", 1)
    tok = query_rows.shape[1]
    nx = lax.axis_size("gx")
    nz = lax.axis_size("gz")
    heads = nx * nz
    kv_heads = key_rows.shape[2] // HEAD_SIZE
    prefill_stretch = tok * heads
    q_rows = query_rows[0].reshape(tok, heads, HEAD_SIZE)
    own_query = lax.all_to_all(
        q_rows, ("gx", "gz"), split_axis=1, concat_axis=0, tiled=True
    ).reshape(prefill_stretch, HEAD_SIZE)

    def stretch_part(rows):
        part = lax.all_to_all(
            rows[0].reshape(tok, kv_heads, HEAD_SIZE), "gx", split_axis=1, concat_axis=0,
            tiled=True,
        )
        gathered = lax.all_gather(part.reshape(nx, tok, HEAD_SIZE), "gz", axis=0, tiled=False)
        return gathered.transpose(1, 0, 2, 3).reshape(prefill_stretch, HEAD_SIZE)

    stretch_k = stretch_part(key_rows)
    stretch_v = stretch_part(value_rows)
    cache_k = lax.all_gather(cache_keys[0, 0], "gz", axis=0, tiled=True)
    cache_v = lax.all_gather(cache_values[0, 0], "gz", axis=0, tiled=True)
    all_k = jnp.concatenate([cache_k, stretch_k], axis=0)
    all_v = jnp.concatenate([cache_v, stretch_v], axis=0)
    result = head_attention(own_query, all_k, all_v, vertical[0, 0], vertical_count[0, 0],
                            slash[0, 0])
    back = lax.all_to_all(
        result.reshape(prefill_stretch, 1, HEAD_SIZE),
        ("gx", "gz"),
        split_axis=0,
        concat_axis=1,
        tiled=True,
    )
    return back.reshape(1, tok, heads * HEAD_SIZE)


def solution(mesh):
    nsec, nseq = mesh.devices.shape
    kv_groups = nseq // GROUP
    grid_mesh = Mesh(mesh.devices.reshape(nsec, kv_groups, GROUP), ("section", "gx", "gz"))
    seq = ("gx", "gz")
    return jax.shard_map(
        per_device,
        mesh=grid_mesh,
        in_specs=(
            P("section", seq, None),
            P("section", seq, None),
            P("section", seq, None),
            P("section", seq, None, None),
            P("section", seq, None, None),
            P("section", seq, None),
            P("section", seq),
            P("section", seq, None),
        ),
        out_specs=P("section", seq, None),
        check_vma=False,
    )
```

```python
import functools
import math

import jax
import jax.numpy as jnp
from jax import lax
from jax.experimental import pallas as pl
from jax.experimental.pallas import tpu as pltpu
from jax.sharding import Mesh
from jax.sharding import PartitionSpec as P

HEAD_SIZE = 128
GROUP = 8
BLK = 64
NVMAX = 32
NS = 11
CACHE = 4096
TQ = 256

big_negative = -1e30


def from_behind(x, axis, by):
    peers = lax.axis_size(axis)
    return lax.ppermute(x, axis, [(i, (i + by) % peers) for i in range(peers)])


def attention_kernel(verts_ref, count_ref, sblk_ref, q_ref, ckv_ref, skv_ref, smask_ref, o_ref,
                     kvert, kslash, *, tok, nz):
    nb = TQ // BLK
    nd = NS + 1
    width = nd * BLK
    nvc = NVMAX * BLK
    tile = pl.program_id(0)
    softmax_scale = 1.0 / math.sqrt(HEAD_SIZE)
    ncb = CACHE // BLK
    per_dev = tok // BLK

    @pl.when(tile == 0)
    def _():
        def fill(s, carry):
            blk = jnp.clip(verts_ref[s], 0, ncb - 1)
            src = pl.multiple_of(blk * BLK, BLK)
            dst = pl.multiple_of(s * BLK, BLK)
            kvert[pl.ds(dst, BLK), :] = ckv_ref[pl.ds(src, BLK), :]
            return carry

        lax.fori_loop(0, NVMAX, fill, 0)

    for b in range(nb):
        qb = tile * nb + b
        for d in range(nd):
            blk = sblk_ref[qb * nd + d]

            @pl.when(blk < ncb)
            def _():
                src = pl.multiple_of(blk * BLK, BLK)
                kslash[b, pl.ds(d * BLK, BLK), :] = ckv_ref[pl.ds(src, BLK), :]

            @pl.when(blk >= ncb)
            def _():
                s = blk - ncb
                dev = s // per_dev
                row = pl.multiple_of((dev // nz) * tok + (s % per_dev) * BLK, BLK)
                kslash[b, pl.ds(d * BLK, BLK), :] = skv_ref[dev % nz, pl.ds(row, BLK), :]

    q = q_ref[...]
    count = count_ref[0]
    s_v = lax.dot_general(q, kvert[:, :HEAD_SIZE], (((1,), (1,)), ((), ())),
                          preferred_element_type=jnp.float32) * softmax_scale
    vcol = lax.broadcasted_iota(jnp.int32, (1, nvc), 1)
    vlive = vcol < count * BLK
    s_v = jnp.where(vlive, s_v, big_negative)
    q3 = q.reshape(nb, BLK, HEAD_SIZE)
    s_s = lax.dot_general(q3, kslash[:, :, :HEAD_SIZE], (((2,), (2,)), ((0,), (0,))),
                          preferred_element_type=jnp.float32) * softmax_scale
    col = lax.broadcasted_iota(jnp.int32, (nb, BLK, width), 2)
    row = lax.broadcasted_iota(jnp.int32, (nb, BLK, width), 1)
    causal = (col >= BLK) | (col <= row)
    smask = (smask_ref[...] > 0) & causal
    s_s = jnp.where(smask, s_s, big_negative)
    top_v = jnp.max(s_v, axis=1, keepdims=True).reshape(nb, BLK, 1)
    top_s = jnp.max(s_s, axis=2, keepdims=True)
    top = jnp.maximum(top_v, top_s)
    p_v = jnp.where(vlive, jnp.exp(s_v - top.reshape(TQ, 1)), 0.0)
    p_s = jnp.where(smask, jnp.exp(s_s - top), 0.0)
    total = jnp.sum(p_v, axis=1, keepdims=True).reshape(nb, BLK, 1) + jnp.sum(
        p_s, axis=2, keepdims=True)
    acc_v = jnp.dot(p_v.astype(jnp.bfloat16), kvert[:, HEAD_SIZE:],
                    preferred_element_type=jnp.float32)
    acc_s = lax.dot_general(p_s.astype(jnp.bfloat16), kslash[:, :, HEAD_SIZE:],
                            (((2,), (1,)), ((0,), (0,))), preferred_element_type=jnp.float32)
    acc = acc_v.reshape(nb, BLK, HEAD_SIZE) + acc_s
    o_ref[...] = (acc / total).reshape(TQ, HEAD_SIZE).astype(o_ref.dtype)


def head_attention(own_query, ckv, skv, verts, count, slashes, tok):
    prefill_stretch = own_query.shape[0]
    nz = skv.shape[0]
    ncb = CACHE // BLK
    nqb = prefill_stretch // BLK
    nd = NS + 1
    offsets = jnp.concatenate([jnp.zeros((1,), jnp.int32), slashes])
    blocks = ncb + jnp.arange(nqb, dtype=jnp.int32)[:, None] - offsets[None, :]
    used = jnp.arange(NVMAX, dtype=jnp.int32)[None, None, :] < count
    listed = jnp.any((blocks[:, :, None] == verts[None, None, :]) & used, axis=2)
    valid = (blocks >= 0) & jnp.logical_not(listed)
    sblk = jnp.clip(blocks, 0, ncb + nqb - 1).reshape(-1)
    smask = jnp.repeat(valid.astype(jnp.int32), BLK, axis=1).reshape(nqb, 1, nd * BLK)
    nb = TQ // BLK
    grid_spec = pltpu.PrefetchScalarGridSpec(
        num_scalar_prefetch=3,
        grid=(prefill_stretch // TQ,),
        in_specs=[
            pl.BlockSpec((TQ, HEAD_SIZE), lambda i, *_: (i, 0)),
            pl.BlockSpec(ckv.shape, lambda i, *_: (0, 0)),
            pl.BlockSpec(skv.shape, lambda i, *_: (0, 0, 0)),
            pl.BlockSpec((nb, 1, nd * BLK), lambda i, *_: (i, 0, 0)),
        ],
        out_specs=pl.BlockSpec((TQ, HEAD_SIZE), lambda i, *_: (i, 0)),
        scratch_shapes=[
            pltpu.VMEM((NVMAX * BLK, 2 * HEAD_SIZE), jnp.bfloat16),
            pltpu.VMEM((nb, nd * BLK, 2 * HEAD_SIZE), jnp.bfloat16),
        ],
    )
    return pl.pallas_call(
        functools.partial(attention_kernel, tok=tok, nz=nz),
        grid_spec=grid_spec,
        out_shape=jax.ShapeDtypeStruct((prefill_stretch, HEAD_SIZE), jnp.bfloat16),
        compiler_params=pltpu.CompilerParams(dimension_semantics=("arbitrary",)),
    )(verts, count.reshape(1), sblk, own_query, ckv, skv, smask)


def per_device(queries, keys, values, cache_keys, cache_values, vertical, vertical_count, slash):
    query_rows, key_rows, value_rows = from_behind((queries, keys, values), "section", 1)
    tok = query_rows.shape[1]
    nx = lax.axis_size("gx")
    nz = lax.axis_size("gz")
    heads = nx * nz
    kv_heads = key_rows.shape[2] // HEAD_SIZE
    prefill_stretch = tok * heads
    q_rows = query_rows[0].reshape(tok, heads, HEAD_SIZE)
    own_query = lax.all_to_all(
        q_rows, ("gx", "gz"), split_axis=1, concat_axis=0, tiled=True
    ).reshape(prefill_stretch, HEAD_SIZE)

    kv_rows = jnp.concatenate(
        [
            key_rows[0].reshape(tok, kv_heads, HEAD_SIZE),
            value_rows[0].reshape(tok, kv_heads, HEAD_SIZE),
        ],
        axis=2,
    )
    part = lax.all_to_all(kv_rows, "gx", split_axis=1, concat_axis=0, tiled=True)
    skv = lax.all_gather(part.reshape(nx * tok, 2 * HEAD_SIZE), "gz", axis=0, tiled=False)
    cache_part = jnp.concatenate([cache_keys[0, 0], cache_values[0, 0]], axis=1)
    ckv = lax.all_gather(cache_part, "gz", axis=0, tiled=True)
    result = head_attention(own_query, ckv, skv, vertical[0, 0], vertical_count[0, 0],
                            slash[0, 0], tok)
    back = lax.all_to_all(
        result.reshape(prefill_stretch, 1, HEAD_SIZE),
        ("gx", "gz"),
        split_axis=0,
        concat_axis=1,
        tiled=True,
    )
    return back.reshape(1, tok, heads * HEAD_SIZE)


def solution(mesh):
    nsec, nseq = mesh.devices.shape
    kv_groups = nseq // GROUP
    grid_mesh = Mesh(mesh.devices.reshape(nsec, kv_groups, GROUP), ("section", "gx", "gz"))
    seq = ("gx", "gz")
    return jax.shard_map(
        per_device,
        mesh=grid_mesh,
        in_specs=(
            P("section", seq, None),
            P("section", seq, None),
            P("section", seq, None),
            P("section", seq, None, None),
            P("section", seq, None, None),
            P("section", seq, None),
            P("section", seq),
            P("section", seq, None),
        ),
        out_specs=P("section", seq, None),
        check_vma=False,
    )
```

```python
import functools
import math

import jax
import jax.numpy as jnp
from jax import lax
from jax.experimental import pallas as pl
from jax.experimental.pallas import tpu as pltpu
from jax.sharding import Mesh
from jax.sharding import PartitionSpec as P

HEAD_SIZE = 128
GROUP = 8
BLK = 64
NVMAX = 32
NS = 11
CACHE = 4096
TQ = 256

big_negative = -1e30


def from_behind(x, axis, by):
    peers = lax.axis_size(axis)
    return lax.ppermute(x, axis, [(i, (i + by) % peers) for i in range(peers)])


def ring_gather(piece, axis):
    peers = lax.axis_size(axis)
    ahead = [(i, (i + 1) % peers) for i in range(peers)]
    behind = [(i, (i - 1) % peers) for i in range(peers)]
    planes = [None] * peers
    planes[0] = piece
    up = piece
    down = piece
    for step in range(1, peers // 2 + 1):
        up = lax.ppermute(up, axis, ahead)
        planes[peers - step] = up
        if step < peers - step:
            down = lax.ppermute(down, axis, behind)
            planes[step] = down
    return jnp.stack(planes)


def attention_kernel(verts_ref, count_ref, sblk_ref, rank_ref, q_ref, ckv_ref, skv_ref, smask_ref, o_ref,
                     kvert, kslash, *, tok, nz):
    nb = TQ // BLK
    nd = NS + 1
    width = nd * BLK
    nvc = NVMAX * BLK
    tile = pl.program_id(0)
    softmax_scale = 1.0 / math.sqrt(HEAD_SIZE)
    ncb = CACHE // BLK
    per_dev = tok // BLK
    rank = rank_ref[0]
    cache_rows = ckv_ref.shape[1]
    cache_per = cache_rows // BLK

    @pl.when(tile == 0)
    def _():
        def fill(s, carry):
            blk = jnp.clip(verts_ref[s], 0, ncb - 1)
            src = pl.multiple_of((blk % cache_per) * BLK, BLK)
            plane = (blk // cache_per - rank + nz) % nz
            dst = pl.multiple_of(s * BLK, BLK)
            kvert[pl.ds(dst, BLK), :] = ckv_ref[plane, pl.ds(src, BLK), :]
            return carry

        lax.fori_loop(0, NVMAX, fill, 0)

    for b in range(nb):
        qb = tile * nb + b
        for d in range(nd):
            blk = sblk_ref[qb * nd + d]

            @pl.when(blk < ncb)
            def _():
                src = pl.multiple_of((blk % cache_per) * BLK, BLK)
                plane = (blk // cache_per - rank + nz) % nz
                kslash[b, pl.ds(d * BLK, BLK), :] = ckv_ref[plane, pl.ds(src, BLK), :]

            @pl.when(blk >= ncb)
            def _():
                s = blk - ncb
                dev = s // per_dev
                row = pl.multiple_of((dev // nz) * tok + (s % per_dev) * BLK, BLK)
                plane = (dev % nz - rank + nz) % nz
                kslash[b, pl.ds(d * BLK, BLK), :] = skv_ref[plane, pl.ds(row, BLK), :]

    q = q_ref[...]
    count = count_ref[0]
    s_v = lax.dot_general(q, kvert[:, :HEAD_SIZE], (((1,), (1,)), ((), ())),
                          preferred_element_type=jnp.float32) * softmax_scale
    vcol = lax.broadcasted_iota(jnp.int32, (1, nvc), 1)
    vlive = vcol < count * BLK
    s_v = jnp.where(vlive, s_v, big_negative)
    q3 = q.reshape(nb, BLK, HEAD_SIZE)
    s_s = lax.dot_general(q3, kslash[:, :, :HEAD_SIZE], (((2,), (2,)), ((0,), (0,))),
                          preferred_element_type=jnp.float32) * softmax_scale
    col = lax.broadcasted_iota(jnp.int32, (nb, BLK, width), 2)
    row = lax.broadcasted_iota(jnp.int32, (nb, BLK, width), 1)
    causal = (col >= BLK) | (col <= row)
    smask = (smask_ref[...] > 0) & causal
    s_s = jnp.where(smask, s_s, big_negative)
    top_v = jnp.max(s_v, axis=1, keepdims=True).reshape(nb, BLK, 1)
    top_s = jnp.max(s_s, axis=2, keepdims=True)
    top = jnp.maximum(top_v, top_s)
    p_v = jnp.where(vlive, jnp.exp(s_v - top.reshape(TQ, 1)), 0.0)
    p_s = jnp.where(smask, jnp.exp(s_s - top), 0.0)
    total = jnp.sum(p_v, axis=1, keepdims=True).reshape(nb, BLK, 1) + jnp.sum(
        p_s, axis=2, keepdims=True)
    acc_v = jnp.dot(p_v.astype(jnp.bfloat16), kvert[:, HEAD_SIZE:],
                    preferred_element_type=jnp.float32)
    acc_s = lax.dot_general(p_s.astype(jnp.bfloat16), kslash[:, :, HEAD_SIZE:],
                            (((2,), (1,)), ((0,), (0,))), preferred_element_type=jnp.float32)
    acc = acc_v.reshape(nb, BLK, HEAD_SIZE) + acc_s
    o_ref[...] = (acc / total).reshape(TQ, HEAD_SIZE).astype(o_ref.dtype)


def head_attention(own_query, ckv, skv, verts, count, slashes, tok, rank):
    prefill_stretch = own_query.shape[0]
    nz = skv.shape[0]
    ncb = CACHE // BLK
    nqb = prefill_stretch // BLK
    nd = NS + 1
    offsets = jnp.concatenate([jnp.zeros((1,), jnp.int32), slashes])
    blocks = ncb + jnp.arange(nqb, dtype=jnp.int32)[:, None] - offsets[None, :]
    used = jnp.arange(NVMAX, dtype=jnp.int32)[None, None, :] < count
    listed = jnp.any((blocks[:, :, None] == verts[None, None, :]) & used, axis=2)
    valid = (blocks >= 0) & jnp.logical_not(listed)
    sblk = jnp.clip(blocks, 0, ncb + nqb - 1).reshape(-1)
    smask = jnp.repeat(valid.astype(jnp.int32), BLK, axis=1).reshape(nqb, 1, nd * BLK)
    nb = TQ // BLK
    grid_spec = pltpu.PrefetchScalarGridSpec(
        num_scalar_prefetch=4,
        grid=(prefill_stretch // TQ,),
        in_specs=[
            pl.BlockSpec((TQ, HEAD_SIZE), lambda i, *_: (i, 0)),
            pl.BlockSpec(ckv.shape, lambda i, *_: (0, 0, 0)),
            pl.BlockSpec(skv.shape, lambda i, *_: (0, 0, 0)),
            pl.BlockSpec((nb, 1, nd * BLK), lambda i, *_: (i, 0, 0)),
        ],
        out_specs=pl.BlockSpec((TQ, HEAD_SIZE), lambda i, *_: (i, 0)),
        scratch_shapes=[
            pltpu.VMEM((NVMAX * BLK, 2 * HEAD_SIZE), jnp.bfloat16),
            pltpu.VMEM((nb, nd * BLK, 2 * HEAD_SIZE), jnp.bfloat16),
        ],
    )
    return pl.pallas_call(
        functools.partial(attention_kernel, tok=tok, nz=nz),
        grid_spec=grid_spec,
        out_shape=jax.ShapeDtypeStruct((prefill_stretch, HEAD_SIZE), jnp.bfloat16),
        compiler_params=pltpu.CompilerParams(dimension_semantics=("arbitrary",)),
    )(verts, count.reshape(1), sblk, rank.reshape(1), own_query, ckv, skv, smask)


def per_device(queries, keys, values, cache_keys, cache_values, vertical, vertical_count, slash):
    query_rows, key_rows, value_rows = from_behind((queries, keys, values), "section", 1)
    tok = query_rows.shape[1]
    nx = lax.axis_size("gx")
    nz = lax.axis_size("gz")
    heads = nx * nz
    kv_heads = key_rows.shape[2] // HEAD_SIZE
    prefill_stretch = tok * heads
    q_rows = query_rows[0].reshape(tok, heads, HEAD_SIZE)
    own_query = lax.all_to_all(
        q_rows, ("gx", "gz"), split_axis=1, concat_axis=0, tiled=True
    ).reshape(prefill_stretch, HEAD_SIZE)

    kv_rows = jnp.concatenate(
        [
            key_rows[0].reshape(tok, kv_heads, HEAD_SIZE),
            value_rows[0].reshape(tok, kv_heads, HEAD_SIZE),
        ],
        axis=2,
    )
    part = lax.all_to_all(kv_rows, "gx", split_axis=1, concat_axis=0, tiled=True)
    cache_part = jnp.concatenate([cache_keys[0, 0], cache_values[0, 0]], axis=1)
    ckv = ring_gather(cache_part, "gz")
    skv = ring_gather(part.reshape(nx * tok, 2 * HEAD_SIZE), "gz")
    rank = lax.axis_index("gz").astype(jnp.int32)
    result = head_attention(own_query, ckv, skv, vertical[0, 0], vertical_count[0, 0],
                            slash[0, 0], tok, rank)
    back = lax.all_to_all(
        result.reshape(prefill_stretch, 1, HEAD_SIZE),
        ("gx", "gz"),
        split_axis=0,
        concat_axis=1,
        tiled=True,
    )
    return back.reshape(1, tok, heads * HEAD_SIZE)


def solution(mesh):
    nsec, nseq = mesh.devices.shape
    kv_groups = nseq // GROUP
    grid_mesh = Mesh(mesh.devices.reshape(nsec, kv_groups, GROUP), ("section", "gx", "gz"))
    seq = ("gx", "gz")
    return jax.shard_map(
        per_device,
        mesh=grid_mesh,
        in_specs=(
            P("section", seq, None),
            P("section", seq, None),
            P("section", seq, None),
            P("section", seq, None, None),
            P("section", seq, None, None),
            P("section", seq, None),
            P("section", seq),
            P("section", seq, None),
        ),
        out_specs=P("section", seq, None),
        check_vma=False,
    )
```

```python
import functools
import math

import jax
import jax.numpy as jnp
from jax import lax
from jax.experimental import pallas as pl
from jax.experimental.pallas import tpu as pltpu
from jax.sharding import Mesh
from jax.sharding import PartitionSpec as P

HEAD_SIZE = 128
GROUP = 8
BLK = 64
NVMAX = 32
NS = 11
CACHE = 4096
TQ = 256

big_negative = -1e30


def from_behind(x, axis, by):
    peers = lax.axis_size(axis)
    return lax.ppermute(x, axis, [(i, (i + by) % peers) for i in range(peers)])


def vertical_kernel(verts_ref, q_ref, ckv_ref, vbias_ref, acc_ref, top_ref, total_ref, kvert):
    tile = pl.program_id(0)
    softmax_scale = 1.0 / math.sqrt(HEAD_SIZE)
    ncb = CACHE // BLK

    @pl.when(tile == 0)
    def _():
        def fill(s, carry):
            blk = jnp.clip(verts_ref[s], 0, ncb - 1)
            src = pl.multiple_of(blk * BLK, BLK)
            dst = pl.multiple_of(s * BLK, BLK)
            kvert[pl.ds(dst, BLK), :] = ckv_ref[pl.ds(src, BLK), :]
            return carry

        lax.fori_loop(0, NVMAX, fill, 0)

    scores = lax.dot_general(q_ref[...], kvert[:, :HEAD_SIZE], (((1,), (1,)), ((), ())),
                             preferred_element_type=jnp.float32) * softmax_scale + vbias_ref[...]
    top = jnp.max(scores, axis=1, keepdims=True)
    weights = jnp.exp(scores - top)
    total_ref[...] = jnp.sum(weights, axis=1, keepdims=True)
    top_ref[...] = top
    acc_ref[...] = jnp.dot(weights.astype(jnp.bfloat16), kvert[:, HEAD_SIZE:],
                           preferred_element_type=jnp.float32)


def slash_kernel(sblk_ref, q_ref, ckv_ref, skv_ref, smask_ref, acc_ref, top_ref, total_ref,
                 o_ref, kslash, *, tok, nz):
    nb = TQ // BLK
    nd = NS + 1
    width = nd * BLK
    tile = pl.program_id(0)
    softmax_scale = 1.0 / math.sqrt(HEAD_SIZE)
    ncb = CACHE // BLK
    per_dev = tok // BLK

    for b in range(nb):
        qb = tile * nb + b
        for d in range(nd):
            blk = sblk_ref[qb * nd + d]

            @pl.when(blk < ncb)
            def _():
                src = pl.multiple_of(blk * BLK, BLK)
                kslash[b, pl.ds(d * BLK, BLK), :] = ckv_ref[pl.ds(src, BLK), :]

            @pl.when(blk >= ncb)
            def _():
                s = blk - ncb
                dev = s // per_dev
                row = pl.multiple_of((dev // nz) * tok + (s % per_dev) * BLK, BLK)
                kslash[b, pl.ds(d * BLK, BLK), :] = skv_ref[dev % nz, pl.ds(row, BLK), :]

    q3 = q_ref[...].reshape(nb, BLK, HEAD_SIZE)
    s_s = lax.dot_general(q3, kslash[:, :, :HEAD_SIZE], (((2,), (2,)), ((0,), (0,))),
                          preferred_element_type=jnp.float32) * softmax_scale
    col = lax.broadcasted_iota(jnp.int32, (nb, BLK, width), 2)
    row = lax.broadcasted_iota(jnp.int32, (nb, BLK, width), 1)
    causal = (col >= BLK) | (col <= row)
    smask = (smask_ref[...] > 0) & causal
    s_s = jnp.where(smask, s_s, big_negative)
    top_v = top_ref[...].reshape(nb, BLK, 1)
    top = jnp.maximum(top_v, jnp.max(s_s, axis=2, keepdims=True))
    factor = jnp.exp(top_v - top)
    p_s = jnp.exp(s_s - top)
    total = total_ref[...].reshape(nb, BLK, 1) * factor + jnp.sum(p_s, axis=2, keepdims=True)
    acc_s = lax.dot_general(p_s.astype(jnp.bfloat16), kslash[:, :, HEAD_SIZE:],
                            (((2,), (1,)), ((0,), (0,))), preferred_element_type=jnp.float32)
    acc = acc_ref[...].reshape(nb, BLK, HEAD_SIZE) * factor + acc_s
    o_ref[...] = (acc / total).reshape(TQ, HEAD_SIZE).astype(o_ref.dtype)


def vertical_part(own_query, ckv, verts, count):
    prefill_stretch = own_query.shape[0]
    nvc = NVMAX * BLK
    slot = jnp.arange(nvc, dtype=jnp.int32) // BLK
    vbias = jnp.where(slot < count, 0.0, big_negative).astype(jnp.float32).reshape(1, nvc)
    grid_spec = pltpu.PrefetchScalarGridSpec(
        num_scalar_prefetch=1,
        grid=(prefill_stretch // TQ,),
        in_specs=[
            pl.BlockSpec((TQ, HEAD_SIZE), lambda i, *_: (i, 0)),
            pl.BlockSpec(ckv.shape, lambda i, *_: (0, 0)),
            pl.BlockSpec((1, nvc), lambda i, *_: (0, 0)),
        ],
        out_specs=[
            pl.BlockSpec((TQ, HEAD_SIZE), lambda i, *_: (i, 0)),
            pl.BlockSpec((TQ, 1), lambda i, *_: (i, 0)),
            pl.BlockSpec((TQ, 1), lambda i, *_: (i, 0)),
        ],
        scratch_shapes=[pltpu.VMEM((nvc, 2 * HEAD_SIZE), jnp.bfloat16)],
    )
    return pl.pallas_call(
        vertical_kernel,
        grid_spec=grid_spec,
        out_shape=[
            jax.ShapeDtypeStruct((prefill_stretch, HEAD_SIZE), jnp.float32),
            jax.ShapeDtypeStruct((prefill_stretch, 1), jnp.float32),
            jax.ShapeDtypeStruct((prefill_stretch, 1), jnp.float32),
        ],
        compiler_params=pltpu.CompilerParams(dimension_semantics=("arbitrary",)),
    )(verts, own_query, ckv, vbias)


def head_attention(own_query, ckv, skv, verts, count, slashes, tok):
    prefill_stretch = own_query.shape[0]
    nz = skv.shape[0]
    ncb = CACHE // BLK
    nqb = prefill_stretch // BLK
    nd = NS + 1
    acc_v, top_v, total_v = vertical_part(own_query, ckv, verts, count)
    offsets = jnp.concatenate([jnp.zeros((1,), jnp.int32), slashes])
    blocks = ncb + jnp.arange(nqb, dtype=jnp.int32)[:, None] - offsets[None, :]
    used = jnp.arange(NVMAX, dtype=jnp.int32)[None, None, :] < count
    listed = jnp.any((blocks[:, :, None] == verts[None, None, :]) & used, axis=2)
    valid = (blocks >= 0) & jnp.logical_not(listed)
    sblk = jnp.clip(blocks, 0, ncb + nqb - 1).reshape(-1)
    smask = jnp.repeat(valid.astype(jnp.int32), BLK, axis=1).reshape(nqb, 1, nd * BLK)
    nb = TQ // BLK
    grid_spec = pltpu.PrefetchScalarGridSpec(
        num_scalar_prefetch=1,
        grid=(prefill_stretch // TQ,),
        in_specs=[
            pl.BlockSpec((TQ, HEAD_SIZE), lambda i, *_: (i, 0)),
            pl.BlockSpec(ckv.shape, lambda i, *_: (0, 0)),
            pl.BlockSpec(skv.shape, lambda i, *_: (0, 0, 0)),
            pl.BlockSpec((nb, 1, nd * BLK), lambda i, *_: (i, 0, 0)),
            pl.BlockSpec((TQ, HEAD_SIZE), lambda i, *_: (i, 0)),
            pl.BlockSpec((TQ, 1), lambda i, *_: (i, 0)),
            pl.BlockSpec((TQ, 1), lambda i, *_: (i, 0)),
        ],
        out_specs=pl.BlockSpec((TQ, HEAD_SIZE), lambda i, *_: (i, 0)),
        scratch_shapes=[pltpu.VMEM((nb, nd * BLK, 2 * HEAD_SIZE), jnp.bfloat16)],
    )
    return pl.pallas_call(
        functools.partial(slash_kernel, tok=tok, nz=nz),
        grid_spec=grid_spec,
        out_shape=jax.ShapeDtypeStruct((prefill_stretch, HEAD_SIZE), jnp.bfloat16),
        compiler_params=pltpu.CompilerParams(dimension_semantics=("arbitrary",)),
    )(sblk, own_query, ckv, skv, smask, acc_v, top_v, total_v)


def per_device(queries, keys, values, cache_keys, cache_values, vertical, vertical_count, slash):
    query_rows, key_rows, value_rows = from_behind((queries, keys, values), "section", 1)
    tok = query_rows.shape[1]
    nx = lax.axis_size("gx")
    nz = lax.axis_size("gz")
    heads = nx * nz
    kv_heads = key_rows.shape[2] // HEAD_SIZE
    prefill_stretch = tok * heads
    q_rows = query_rows[0].reshape(tok, heads, HEAD_SIZE)
    own_query = lax.all_to_all(
        q_rows, ("gx", "gz"), split_axis=1, concat_axis=0, tiled=True
    ).reshape(prefill_stretch, HEAD_SIZE)

    kv_rows = jnp.concatenate(
        [
            key_rows[0].reshape(tok, kv_heads, HEAD_SIZE),
            value_rows[0].reshape(tok, kv_heads, HEAD_SIZE),
        ],
        axis=2,
    )
    part = lax.all_to_all(kv_rows, "gx", split_axis=1, concat_axis=0, tiled=True)
    skv = lax.all_gather(part.reshape(nx * tok, 2 * HEAD_SIZE), "gz", axis=0, tiled=False)
    cache_part = jnp.concatenate([cache_keys[0, 0], cache_values[0, 0]], axis=1)
    ckv = lax.all_gather(cache_part, "gz", axis=0, tiled=True)
    result = head_attention(own_query, ckv, skv, vertical[0, 0], vertical_count[0, 0],
                            slash[0, 0], tok)
    back = lax.all_to_all(
        result.reshape(prefill_stretch, 1, HEAD_SIZE),
        ("gx", "gz"),
        split_axis=0,
        concat_axis=1,
        tiled=True,
    )
    return back.reshape(1, tok, heads * HEAD_SIZE)


def solution(mesh):
    nsec, nseq = mesh.devices.shape
    kv_groups = nseq // GROUP
    grid_mesh = Mesh(mesh.devices.reshape(nsec, kv_groups, GROUP), ("section", "gx", "gz"))
    seq = ("gx", "gz")
    return jax.shard_map(
        per_device,
        mesh=grid_mesh,
        in_specs=(
            P("section", seq, None),
            P("section", seq, None),
            P("section", seq, None),
            P("section", seq, None, None),
            P("section", seq, None, None),
            P("section", seq, None),
            P("section", seq),
            P("section", seq, None),
        ),
        out_specs=P("section", seq, None),
        check_vma=False,
    )
```

```python
import functools
import math

import jax
import jax.numpy as jnp
from jax import lax
from jax.experimental import pallas as pl
from jax.experimental.pallas import tpu as pltpu
from jax.sharding import Mesh
from jax.sharding import PartitionSpec as P

HEAD_SIZE = 128
GROUP = 8
BLK = 64
NVMAX = 32
NS = 11
CACHE = 4096
TQ = 256

big_negative = -1e30


def from_behind(x, axis, by):
    peers = lax.axis_size(axis)
    return lax.ppermute(x, axis, [(i, (i + by) % peers) for i in range(peers)])


def vertical_kernel(verts_ref, q_ref, ckv_ref, vbias_ref, acc_ref, top_ref, total_ref, kvert):
    tile = pl.program_id(0)
    softmax_scale = 1.0 / math.sqrt(HEAD_SIZE)
    ncb = CACHE // BLK

    @pl.when(tile == 0)
    def _():
        def fill(s, carry):
            blk = jnp.clip(verts_ref[s], 0, ncb - 1)
            src = pl.multiple_of(blk * BLK, BLK)
            dst = pl.multiple_of(s * BLK, BLK)
            kvert[pl.ds(dst, BLK), :] = ckv_ref[pl.ds(src, BLK), :]
            return carry

        lax.fori_loop(0, NVMAX, fill, 0)

    scores = lax.dot_general(q_ref[...], kvert[:, :HEAD_SIZE], (((1,), (1,)), ((), ())),
                             preferred_element_type=jnp.float32) * softmax_scale + vbias_ref[...]
    top = jnp.max(scores, axis=1, keepdims=True)
    weights = jnp.exp(scores - top)
    total_ref[...] = jnp.sum(weights, axis=1, keepdims=True)
    top_ref[...] = top
    acc_ref[...] = jnp.dot(weights.astype(jnp.bfloat16), kvert[:, HEAD_SIZE:],
                           preferred_element_type=jnp.float32)


def slash_kernel(crow_ref, splane_ref, srow_ref, pick_ref, q_ref, ckv_ref, skv_ref, sbias_ref,
                 acc_ref, top_ref, total_ref, o_ref, kslash, causal_bias):
    nb = TQ // BLK
    nd = NS + 1
    width = nd * BLK
    tile = pl.program_id(0)
    softmax_scale = 1.0 / math.sqrt(HEAD_SIZE)

    @pl.when(tile == 0)
    def _():
        col = lax.broadcasted_iota(jnp.int32, (BLK, width), 1)
        row = lax.broadcasted_iota(jnp.int32, (BLK, width), 0)
        causal = (col >= BLK) | (col <= row)
        causal_bias[...] = jnp.where(causal, 0.0, big_negative).astype(jnp.float32)

    for b in range(nb):
        qb = tile * nb + b
        for d in range(nd):
            at = qb * nd + d
            from_cache = ckv_ref[pl.ds(pl.multiple_of(crow_ref[at], BLK), BLK), :]
            from_stretch = skv_ref[splane_ref[at], pl.ds(pl.multiple_of(srow_ref[at], BLK), BLK), :]
            kslash[b, pl.ds(d * BLK, BLK), :] = jnp.where(pick_ref[at] > 0, from_stretch,
                                                          from_cache)

    q3 = q_ref[...].reshape(nb, BLK, HEAD_SIZE)
    s_s = lax.dot_general(q3, kslash[:, :, :HEAD_SIZE], (((2,), (2,)), ((0,), (0,))),
                          preferred_element_type=jnp.float32) * softmax_scale
    s_s = s_s + sbias_ref[...] + causal_bias[...][None, :, :]
    top_v = top_ref[...].reshape(nb, BLK, 1)
    top = jnp.maximum(top_v, jnp.max(s_s, axis=2, keepdims=True))
    factor = jnp.exp(top_v - top)
    p_s = jnp.exp(s_s - top)
    total = total_ref[...].reshape(nb, BLK, 1) * factor + jnp.sum(p_s, axis=2, keepdims=True)
    acc_s = lax.dot_general(p_s.astype(jnp.bfloat16), kslash[:, :, HEAD_SIZE:],
                            (((2,), (1,)), ((0,), (0,))), preferred_element_type=jnp.float32)
    acc = acc_ref[...].reshape(nb, BLK, HEAD_SIZE) * factor + acc_s
    o_ref[...] = (acc / total).reshape(TQ, HEAD_SIZE).astype(o_ref.dtype)


def vertical_part(own_query, ckv, verts, count):
    prefill_stretch = own_query.shape[0]
    nvc = NVMAX * BLK
    slot = jnp.arange(nvc, dtype=jnp.int32) // BLK
    vbias = jnp.where(slot < count, 0.0, big_negative).astype(jnp.float32).reshape(1, nvc)
    grid_spec = pltpu.PrefetchScalarGridSpec(
        num_scalar_prefetch=1,
        grid=(prefill_stretch // TQ,),
        in_specs=[
            pl.BlockSpec((TQ, HEAD_SIZE), lambda i, *_: (i, 0)),
            pl.BlockSpec(ckv.shape, lambda i, *_: (0, 0)),
            pl.BlockSpec((1, nvc), lambda i, *_: (0, 0)),
        ],
        out_specs=[
            pl.BlockSpec((TQ, HEAD_SIZE), lambda i, *_: (i, 0)),
            pl.BlockSpec((TQ, 1), lambda i, *_: (i, 0)),
            pl.BlockSpec((TQ, 1), lambda i, *_: (i, 0)),
        ],
        scratch_shapes=[pltpu.VMEM((nvc, 2 * HEAD_SIZE), jnp.bfloat16)],
    )
    return pl.pallas_call(
        vertical_kernel,
        grid_spec=grid_spec,
        out_shape=[
            jax.ShapeDtypeStruct((prefill_stretch, HEAD_SIZE), jnp.float32),
            jax.ShapeDtypeStruct((prefill_stretch, 1), jnp.float32),
            jax.ShapeDtypeStruct((prefill_stretch, 1), jnp.float32),
        ],
        compiler_params=pltpu.CompilerParams(dimension_semantics=("arbitrary",)),
    )(verts, own_query, ckv, vbias)


def head_attention(own_query, ckv, skv, verts, count, slashes, tok):
    prefill_stretch = own_query.shape[0]
    nz = skv.shape[0]
    ncb = CACHE // BLK
    nqb = prefill_stretch // BLK
    nd = NS + 1
    acc_v, top_v, total_v = vertical_part(own_query, ckv, verts, count)
    offsets = jnp.concatenate([jnp.zeros((1,), jnp.int32), slashes])
    blocks = ncb + jnp.arange(nqb, dtype=jnp.int32)[:, None] - offsets[None, :]
    used = jnp.arange(NVMAX, dtype=jnp.int32)[None, None, :] < count
    listed = jnp.any((blocks[:, :, None] == verts[None, None, :]) & used, axis=2)
    valid = (blocks >= 0) & jnp.logical_not(listed)
    per_dev = tok // BLK
    stretch_blk = jnp.clip(blocks - ncb, 0, nqb - 1)
    dev = stretch_blk // per_dev
    pick = (blocks >= ncb).astype(jnp.int32).reshape(-1)
    crow = (jnp.clip(blocks, 0, ncb - 1) * BLK).reshape(-1)
    splane = (dev % nz).reshape(-1)
    srow = ((dev // nz) * tok + (stretch_blk % per_dev) * BLK).reshape(-1)
    sbias = jnp.repeat(jnp.where(valid, 0.0, big_negative).astype(jnp.float32), BLK,
                       axis=1).reshape(nqb, 1, nd * BLK)
    nb = TQ // BLK
    grid_spec = pltpu.PrefetchScalarGridSpec(
        num_scalar_prefetch=4,
        grid=(prefill_stretch // TQ,),
        in_specs=[
            pl.BlockSpec((TQ, HEAD_SIZE), lambda i, *_: (i, 0)),
            pl.BlockSpec(ckv.shape, lambda i, *_: (0, 0)),
            pl.BlockSpec(skv.shape, lambda i, *_: (0, 0, 0)),
            pl.BlockSpec((nb, 1, nd * BLK), lambda i, *_: (i, 0, 0)),
            pl.BlockSpec((TQ, HEAD_SIZE), lambda i, *_: (i, 0)),
            pl.BlockSpec((TQ, 1), lambda i, *_: (i, 0)),
            pl.BlockSpec((TQ, 1), lambda i, *_: (i, 0)),
        ],
        out_specs=pl.BlockSpec((TQ, HEAD_SIZE), lambda i, *_: (i, 0)),
        scratch_shapes=[
            pltpu.VMEM((nb, nd * BLK, 2 * HEAD_SIZE), jnp.bfloat16),
            pltpu.VMEM((BLK, nd * BLK), jnp.float32),
        ],
    )
    return pl.pallas_call(
        slash_kernel,
        grid_spec=grid_spec,
        out_shape=jax.ShapeDtypeStruct((prefill_stretch, HEAD_SIZE), jnp.bfloat16),
        compiler_params=pltpu.CompilerParams(dimension_semantics=("arbitrary",)),
    )(crow, splane, srow, pick, own_query, ckv, skv, sbias, acc_v, top_v, total_v)


def per_device(queries, keys, values, cache_keys, cache_values, vertical, vertical_count, slash):
    query_rows, key_rows, value_rows = from_behind((queries, keys, values), "section", 1)
    tok = query_rows.shape[1]
    nx = lax.axis_size("gx")
    nz = lax.axis_size("gz")
    heads = nx * nz
    kv_heads = key_rows.shape[2] // HEAD_SIZE
    prefill_stretch = tok * heads
    q_rows = query_rows[0].reshape(tok, heads, HEAD_SIZE)
    own_query = lax.all_to_all(
        q_rows, ("gx", "gz"), split_axis=1, concat_axis=0, tiled=True
    ).reshape(prefill_stretch, HEAD_SIZE)

    kv_rows = jnp.concatenate(
        [
            key_rows[0].reshape(tok, kv_heads, HEAD_SIZE),
            value_rows[0].reshape(tok, kv_heads, HEAD_SIZE),
        ],
        axis=2,
    )
    part = lax.all_to_all(kv_rows, "gx", split_axis=1, concat_axis=0, tiled=True)
    skv = lax.all_gather(part.reshape(nx * tok, 2 * HEAD_SIZE), "gz", axis=0, tiled=False)
    cache_part = jnp.concatenate([cache_keys[0, 0], cache_values[0, 0]], axis=1)
    ckv = lax.all_gather(cache_part, "gz", axis=0, tiled=True)
    result = head_attention(own_query, ckv, skv, vertical[0, 0], vertical_count[0, 0],
                            slash[0, 0], tok)
    back = lax.all_to_all(
        result.reshape(prefill_stretch, 1, HEAD_SIZE),
        ("gx", "gz"),
        split_axis=0,
        concat_axis=1,
        tiled=True,
    )
    return back.reshape(1, tok, heads * HEAD_SIZE)


def solution(mesh):
    nsec, nseq = mesh.devices.shape
    kv_groups = nseq // GROUP
    grid_mesh = Mesh(mesh.devices.reshape(nsec, kv_groups, GROUP), ("section", "gx", "gz"))
    seq = ("gx", "gz")
    return jax.shard_map(
        per_device,
        mesh=grid_mesh,
        in_specs=(
            P("section", seq, None),
            P("section", seq, None),
            P("section", seq, None),
            P("section", seq, None, None),
            P("section", seq, None, None),
            P("section", seq, None),
            P("section", seq),
            P("section", seq, None),
        ),
        out_specs=P("section", seq, None),
        check_vma=False,
    )
```

```python
import functools
import math

import jax
import jax.numpy as jnp
from jax import lax
from jax.experimental import pallas as pl
from jax.experimental.pallas import tpu as pltpu
from jax.sharding import Mesh
from jax.sharding import PartitionSpec as P

HEAD_SIZE = 128
GROUP = 8
BLK = 64
NVMAX = 32
NS = 11
CACHE = 4096
TQ = 256

big_negative = -1e30


def from_behind(x, axis, by):
    peers = lax.axis_size(axis)
    return lax.ppermute(x, axis, [(i, (i + by) % peers) for i in range(peers)])


def vertical_kernel(verts_ref, q_ref, ckv_ref, vbias_ref, acc_ref, top_ref, total_ref, kvert):
    tile = pl.program_id(0)
    softmax_scale = 1.0 / math.sqrt(HEAD_SIZE)
    ncb = CACHE // BLK

    @pl.when(tile == 0)
    def _():
        def fill(s, carry):
            blk = jnp.clip(verts_ref[s], 0, ncb - 1)
            src = pl.multiple_of(blk * BLK, BLK)
            dst = pl.multiple_of(s * BLK, BLK)
            kvert[pl.ds(dst, BLK), :] = ckv_ref[pl.ds(src, BLK), :]
            return carry

        lax.fori_loop(0, NVMAX, fill, 0)

    scores = lax.dot_general(q_ref[...], kvert[:, :HEAD_SIZE], (((1,), (1,)), ((), ())),
                             preferred_element_type=jnp.float32) * softmax_scale + vbias_ref[...]
    top = jnp.max(scores, axis=1, keepdims=True)
    weights = jnp.exp(scores - top)
    total_ref[...] = jnp.sum(weights, axis=1, keepdims=True)
    top_ref[...] = top
    acc_ref[...] = jnp.dot(weights.astype(jnp.bfloat16), kvert[:, HEAD_SIZE:],
                           preferred_element_type=jnp.float32)


def slash_kernel(crow_ref, splane_ref, srow_ref, pick_ref, q_ref, ckv_ref, skv_ref, sbias_ref,
                 acc_ref, top_ref, total_ref, o_ref, kslash, causal_bias, *, parity):
    nb = TQ // BLK
    nd = NS + 1
    width = nd * BLK
    tile = pl.program_id(0)
    softmax_scale = 1.0 / math.sqrt(HEAD_SIZE)

    @pl.when(tile == 0)
    def _():
        col = lax.broadcasted_iota(jnp.int32, (BLK, width), 1)
        row = lax.broadcasted_iota(jnp.int32, (BLK, width), 0)
        causal = (col >= BLK) | (col <= row)
        causal_bias[...] = jnp.where(causal, 0.0, big_negative).astype(jnp.float32)

    for b in range(nb):
        qb = 2 * (tile * nb + b) + parity
        for d in range(nd):
            at = qb * nd + d
            from_cache = ckv_ref[pl.ds(pl.multiple_of(crow_ref[at], BLK), BLK), :]
            from_stretch = skv_ref[splane_ref[at], pl.ds(pl.multiple_of(srow_ref[at], BLK), BLK), :]
            kslash[b, pl.ds(d * BLK, BLK), :] = jnp.where(pick_ref[at] > 0, from_stretch,
                                                          from_cache)

    q3 = q_ref[...].reshape(nb, BLK, HEAD_SIZE)
    s_s = lax.dot_general(q3, kslash[:, :, :HEAD_SIZE], (((2,), (2,)), ((0,), (0,))),
                          preferred_element_type=jnp.float32) * softmax_scale
    s_s = s_s + sbias_ref[...].reshape(nb, 1, width) + causal_bias[...][None, :, :]
    top_v = top_ref[...].reshape(nb, BLK, 1)
    top = jnp.maximum(top_v, jnp.max(s_s, axis=2, keepdims=True))
    factor = jnp.exp(top_v - top)
    p_s = jnp.exp(s_s - top)
    total = total_ref[...].reshape(nb, BLK, 1) * factor + jnp.sum(p_s, axis=2, keepdims=True)
    acc_s = lax.dot_general(p_s.astype(jnp.bfloat16), kslash[:, :, HEAD_SIZE:],
                            (((2,), (1,)), ((0,), (0,))), preferred_element_type=jnp.float32)
    acc = acc_ref[...].reshape(nb, BLK, HEAD_SIZE) * factor + acc_s
    o_ref[...] = (acc / total).astype(o_ref.dtype)


def vertical_part(own_query, ckv, verts, count):
    prefill_stretch = own_query.shape[0]
    nvc = NVMAX * BLK
    slot = jnp.arange(nvc, dtype=jnp.int32) // BLK
    vbias = jnp.where(slot < count, 0.0, big_negative).astype(jnp.float32).reshape(1, nvc)
    grid_spec = pltpu.PrefetchScalarGridSpec(
        num_scalar_prefetch=1,
        grid=(prefill_stretch // TQ,),
        in_specs=[
            pl.BlockSpec((TQ, HEAD_SIZE), lambda i, *_: (i, 0)),
            pl.BlockSpec(ckv.shape, lambda i, *_: (0, 0)),
            pl.BlockSpec((1, nvc), lambda i, *_: (0, 0)),
        ],
        out_specs=[
            pl.BlockSpec((TQ, HEAD_SIZE), lambda i, *_: (i, 0)),
            pl.BlockSpec((TQ, 1), lambda i, *_: (i, 0)),
            pl.BlockSpec((TQ, 1), lambda i, *_: (i, 0)),
        ],
        scratch_shapes=[pltpu.VMEM((nvc, 2 * HEAD_SIZE), jnp.bfloat16)],
    )
    return pl.pallas_call(
        vertical_kernel,
        grid_spec=grid_spec,
        out_shape=[
            jax.ShapeDtypeStruct((prefill_stretch, HEAD_SIZE), jnp.float32),
            jax.ShapeDtypeStruct((prefill_stretch, 1), jnp.float32),
            jax.ShapeDtypeStruct((prefill_stretch, 1), jnp.float32),
        ],
        compiler_params=pltpu.CompilerParams(dimension_semantics=("arbitrary",)),
    )(verts, own_query, ckv, vbias)


def head_attention(own_query, ckv, skv, verts, count, slashes, tok):
    prefill_stretch = own_query.shape[0]
    nz = skv.shape[0]
    ncb = CACHE // BLK
    nqb = prefill_stretch // BLK
    nd = NS + 1
    acc_v, top_v, total_v = vertical_part(own_query, ckv, verts, count)
    offsets = jnp.concatenate([jnp.zeros((1,), jnp.int32), slashes])
    blocks = ncb + jnp.arange(nqb, dtype=jnp.int32)[:, None] - offsets[None, :]
    used = jnp.arange(NVMAX, dtype=jnp.int32)[None, None, :] < count
    listed = jnp.any((blocks[:, :, None] == verts[None, None, :]) & used, axis=2)
    valid = (blocks >= 0) & jnp.logical_not(listed)
    per_dev = tok // BLK
    stretch_blk = jnp.clip(blocks - ncb, 0, nqb - 1)
    dev = stretch_blk // per_dev
    pick = (blocks >= ncb).astype(jnp.int32).reshape(-1)
    crow = (jnp.clip(blocks, 0, ncb - 1) * BLK).reshape(-1)
    splane = (dev % nz).reshape(-1)
    srow = ((dev // nz) * tok + (stretch_blk % per_dev) * BLK).reshape(-1)
    sbias = jnp.repeat(jnp.where(valid, 0.0, big_negative).astype(jnp.float32), BLK,
                       axis=1).reshape(nqb, 1, nd * BLK)
    nb = TQ // BLK
    width = nd * BLK
    halves = nqb // 2
    q4 = own_query.reshape(halves, 2, BLK, HEAD_SIZE)
    acc4 = acc_v.reshape(halves, 2, BLK, HEAD_SIZE)
    top4 = top_v.reshape(halves, 2, BLK, 1)
    total4 = total_v.reshape(halves, 2, BLK, 1)
    sbias4 = sbias.reshape(halves, 2, 1, width)
    outs = []
    for parity in range(2):
        grid_spec = pltpu.PrefetchScalarGridSpec(
            num_scalar_prefetch=4,
            grid=(halves // nb,),
            in_specs=[
                pl.BlockSpec((nb, 1, BLK, HEAD_SIZE), lambda i, *_, p=parity: (i, p, 0, 0)),
                pl.BlockSpec(ckv.shape, lambda i, *_: (0, 0)),
                pl.BlockSpec(skv.shape, lambda i, *_: (0, 0, 0)),
                pl.BlockSpec((nb, 1, 1, width), lambda i, *_, p=parity: (i, p, 0, 0)),
                pl.BlockSpec((nb, 1, BLK, HEAD_SIZE), lambda i, *_, p=parity: (i, p, 0, 0)),
                pl.BlockSpec((nb, 1, BLK, 1), lambda i, *_, p=parity: (i, p, 0, 0)),
                pl.BlockSpec((nb, 1, BLK, 1), lambda i, *_, p=parity: (i, p, 0, 0)),
            ],
            out_specs=pl.BlockSpec((nb, BLK, HEAD_SIZE), lambda i, *_: (i, 0, 0)),
            scratch_shapes=[
                pltpu.VMEM((nb, width, 2 * HEAD_SIZE), jnp.bfloat16),
                pltpu.VMEM((BLK, width), jnp.float32),
            ],
        )
        outs.append(pl.pallas_call(
            functools.partial(slash_kernel, parity=parity),
            grid_spec=grid_spec,
            out_shape=jax.ShapeDtypeStruct((halves, BLK, HEAD_SIZE), jnp.bfloat16),
            compiler_params=pltpu.CompilerParams(dimension_semantics=("arbitrary",)),
        )(crow, splane, srow, pick, q4, ckv, skv, sbias4, acc4, top4, total4))
    return outs


def per_device(queries, keys, values, cache_keys, cache_values, vertical, vertical_count, slash):
    query_rows, key_rows, value_rows = from_behind((queries, keys, values), "section", 1)
    tok = query_rows.shape[1]
    nx = lax.axis_size("gx")
    nz = lax.axis_size("gz")
    heads = nx * nz
    kv_heads = key_rows.shape[2] // HEAD_SIZE
    prefill_stretch = tok * heads
    q_rows = query_rows[0].reshape(tok, heads, HEAD_SIZE)
    own_query = lax.all_to_all(
        q_rows, ("gx", "gz"), split_axis=1, concat_axis=0, tiled=True
    ).reshape(prefill_stretch, HEAD_SIZE)

    kv_rows = jnp.concatenate(
        [
            key_rows[0].reshape(tok, kv_heads, HEAD_SIZE),
            value_rows[0].reshape(tok, kv_heads, HEAD_SIZE),
        ],
        axis=2,
    )
    part = lax.all_to_all(kv_rows, "gx", split_axis=1, concat_axis=0, tiled=True)
    skv = lax.all_gather(part.reshape(nx * tok, 2 * HEAD_SIZE), "gz", axis=0, tiled=False)
    cache_part = jnp.concatenate([cache_keys[0, 0], cache_values[0, 0]], axis=1)
    ckv = lax.all_gather(cache_part, "gz", axis=0, tiled=True)
    halves = head_attention(own_query, ckv, skv, vertical[0, 0], vertical_count[0, 0],
                            slash[0, 0], tok)
    pieces = []
    for half in halves:
        moved = lax.all_to_all(half[:, :, None, :], ("gx", "gz"), split_axis=0, concat_axis=2,
                               tiled=True)
        pieces.append(moved.reshape(tok // 2, heads * HEAD_SIZE))
    return jnp.concatenate(pieces, axis=0).reshape(1, tok, heads * HEAD_SIZE)


def solution(mesh):
    nsec, nseq = mesh.devices.shape
    kv_groups = nseq // GROUP
    grid_mesh = Mesh(mesh.devices.reshape(nsec, kv_groups, GROUP), ("section", "gx", "gz"))
    seq = ("gx", "gz")
    return jax.shard_map(
        per_device,
        mesh=grid_mesh,
        in_specs=(
            P("section", seq, None),
            P("section", seq, None),
            P("section", seq, None),
            P("section", seq, None, None),
            P("section", seq, None, None),
            P("section", seq, None),
            P("section", seq),
            P("section", seq, None),
        ),
        out_specs=P("section", seq, None),
        check_vma=False,
    )
```

```python
import functools
import math

import jax
import jax.numpy as jnp
from jax import lax
from jax.experimental import pallas as pl
from jax.experimental.pallas import tpu as pltpu
from jax.sharding import Mesh
from jax.sharding import PartitionSpec as P

HEAD_SIZE = 128
GROUP = 8
BLK = 64
NVMAX = 32
NS = 11
CACHE = 4096
TQ = 256

big_negative = -1e30


def from_behind(x, axis, by):
    peers = lax.axis_size(axis)
    return lax.ppermute(x, axis, [(i, (i + by) % peers) for i in range(peers)])


def vertical_kernel(verts_ref, q_ref, ckv_ref, vbias_ref, acc_ref, top_ref, total_ref, kvert):
    tile = pl.program_id(0)
    softmax_scale = 1.0 / math.sqrt(HEAD_SIZE)
    ncb = CACHE // BLK

    @pl.when(tile == 0)
    def _():
        def fill(s, carry):
            blk = jnp.clip(verts_ref[s], 0, ncb - 1)
            src = pl.multiple_of(blk * BLK, BLK)
            dst = pl.multiple_of(s * BLK, BLK)
            kvert[pl.ds(dst, BLK), :] = ckv_ref[pl.ds(src, BLK), :]
            return carry

        lax.fori_loop(0, NVMAX, fill, 0)

    scores = lax.dot_general(q_ref[...], kvert[:, :HEAD_SIZE], (((1,), (1,)), ((), ())),
                             preferred_element_type=jnp.float32) * softmax_scale + vbias_ref[...]
    top = jnp.max(scores, axis=1, keepdims=True)
    weights = jnp.exp(scores - top)
    total_ref[...] = jnp.sum(weights, axis=1, keepdims=True)
    top_ref[...] = top
    acc_ref[...] = jnp.dot(weights.astype(jnp.bfloat16), kvert[:, HEAD_SIZE:],
                           preferred_element_type=jnp.float32)


def slash_kernel(crow_ref, splane_ref, srow_ref, pick_ref, q_ref, ckv_ref, skv_ref, sbias_ref,
                 acc_ref, top_ref, total_ref, o_ref, kslash, causal_bias, *, parity):
    nb = TQ // BLK
    nd = NS + 1
    width = nd * BLK
    tile = pl.program_id(0)
    softmax_scale = 1.0 / math.sqrt(HEAD_SIZE)

    @pl.when(tile == 0)
    def _():
        col = lax.broadcasted_iota(jnp.int32, (BLK, width), 1)
        row = lax.broadcasted_iota(jnp.int32, (BLK, width), 0)
        causal = (col >= BLK) | (col <= row)
        causal_bias[...] = jnp.where(causal, 0.0, big_negative).astype(jnp.float32)

    for b in range(nb):
        qb = 2 * (tile * nb + b) + parity
        for d in range(nd):
            at = qb * nd + d
            from_cache = ckv_ref[pl.ds(pl.multiple_of(crow_ref[at], BLK), BLK), :]
            from_stretch = skv_ref[splane_ref[at], pl.ds(pl.multiple_of(srow_ref[at], BLK), BLK), :]
            kslash[b, pl.ds(d * BLK, BLK), :] = jnp.where(pick_ref[at] > 0, from_stretch,
                                                          from_cache)

    q3 = q_ref[...].reshape(nb, BLK, HEAD_SIZE)
    s_s = lax.dot_general(q3, kslash[:, :, :HEAD_SIZE], (((2,), (2,)), ((0,), (0,))),
                          preferred_element_type=jnp.float32) * softmax_scale
    s_s = s_s + sbias_ref[...].reshape(nb, 1, width) + causal_bias[...][None, :, :]
    top_v = top_ref[...].reshape(nb, BLK, 1)
    top = jnp.maximum(top_v, jnp.max(s_s, axis=2, keepdims=True))
    factor = jnp.exp(top_v - top)
    p_s = jnp.exp(s_s - top)
    total = total_ref[...].reshape(nb, BLK, 1) * factor + jnp.sum(p_s, axis=2, keepdims=True)
    acc_s = lax.dot_general(p_s.astype(jnp.bfloat16), kslash[:, :, HEAD_SIZE:],
                            (((2,), (1,)), ((0,), (0,))), preferred_element_type=jnp.float32)
    acc = acc_ref[...].reshape(nb, BLK, HEAD_SIZE) * factor + acc_s
    o_ref[...] = (acc / total).astype(o_ref.dtype)


def vertical_part(own_query, ckv, verts, count):
    prefill_stretch = own_query.shape[0]
    nvc = NVMAX * BLK
    slot = jnp.arange(nvc, dtype=jnp.int32) // BLK
    vbias = jnp.where(slot < count, 0.0, big_negative).astype(jnp.float32).reshape(1, nvc)
    grid_spec = pltpu.PrefetchScalarGridSpec(
        num_scalar_prefetch=1,
        grid=(prefill_stretch // TQ,),
        in_specs=[
            pl.BlockSpec((TQ, HEAD_SIZE), lambda i, *_: (i, 0)),
            pl.BlockSpec(ckv.shape, lambda i, *_: (0, 0)),
            pl.BlockSpec((1, nvc), lambda i, *_: (0, 0)),
        ],
        out_specs=[
            pl.BlockSpec((TQ, HEAD_SIZE), lambda i, *_: (i, 0)),
            pl.BlockSpec((TQ, 1), lambda i, *_: (i, 0)),
            pl.BlockSpec((TQ, 1), lambda i, *_: (i, 0)),
        ],
        scratch_shapes=[pltpu.VMEM((nvc, 2 * HEAD_SIZE), jnp.bfloat16)],
    )
    return pl.pallas_call(
        vertical_kernel,
        grid_spec=grid_spec,
        out_shape=[
            jax.ShapeDtypeStruct((prefill_stretch, HEAD_SIZE), jnp.float32),
            jax.ShapeDtypeStruct((prefill_stretch, 1), jnp.float32),
            jax.ShapeDtypeStruct((prefill_stretch, 1), jnp.float32),
        ],
        compiler_params=pltpu.CompilerParams(dimension_semantics=("arbitrary",)),
    )(verts, own_query, ckv, vbias)


def head_attention(own_query, ckv, skv, verts, count, slashes, tok):
    prefill_stretch = own_query.shape[0]
    nz = skv.shape[0]
    ncb = CACHE // BLK
    nqb = prefill_stretch // BLK
    nd = NS + 1
    acc_v, top_v, total_v = vertical_part(own_query, ckv, verts, count)
    offsets = jnp.concatenate([jnp.zeros((1,), jnp.int32), slashes])
    blocks = ncb + jnp.arange(nqb, dtype=jnp.int32)[:, None] - offsets[None, :]
    used = jnp.arange(NVMAX, dtype=jnp.int32)[None, None, :] < count
    listed = jnp.any((blocks[:, :, None] == verts[None, None, :]) & used, axis=2)
    valid = (blocks >= 0) & jnp.logical_not(listed)
    per_dev = tok // BLK
    stretch_blk = jnp.clip(blocks - ncb, 0, nqb - 1)
    dev = stretch_blk // per_dev
    pick = (blocks >= ncb).astype(jnp.int32).reshape(-1)
    crow = (jnp.clip(blocks, 0, ncb - 1) * BLK).reshape(-1)
    splane = (dev % nz).reshape(-1)
    srow = ((dev // nz) * tok + (stretch_blk % per_dev) * BLK).reshape(-1)
    sbias = jnp.repeat(jnp.where(valid, 0.0, big_negative).astype(jnp.float32), BLK,
                       axis=1).reshape(nqb, 1, nd * BLK)
    nb = TQ // BLK
    width = nd * BLK
    halves = nqb // 2
    q4 = own_query.reshape(halves, 2, BLK, HEAD_SIZE)
    acc4 = acc_v.reshape(halves, 2, BLK, HEAD_SIZE)
    top4 = top_v.reshape(halves, 2, BLK, 1)
    total4 = total_v.reshape(halves, 2, BLK, 1)
    sbias4 = sbias.reshape(halves, 2, 1, width)
    outs = []
    for parity in range(2):
        grid_spec = pltpu.PrefetchScalarGridSpec(
            num_scalar_prefetch=4,
            grid=(halves // nb,),
            in_specs=[
                pl.BlockSpec((nb, 1, BLK, HEAD_SIZE), lambda i, *_, p=parity: (i, p, 0, 0)),
                pl.BlockSpec(ckv.shape, lambda i, *_: (0, 0)),
                pl.BlockSpec(skv.shape, lambda i, *_: (0, 0, 0)),
                pl.BlockSpec((nb, 1, 1, width), lambda i, *_, p=parity: (i, p, 0, 0)),
                pl.BlockSpec((nb, 1, BLK, HEAD_SIZE), lambda i, *_, p=parity: (i, p, 0, 0)),
                pl.BlockSpec((nb, 1, BLK, 1), lambda i, *_, p=parity: (i, p, 0, 0)),
                pl.BlockSpec((nb, 1, BLK, 1), lambda i, *_, p=parity: (i, p, 0, 0)),
            ],
            out_specs=pl.BlockSpec((nb, BLK, HEAD_SIZE), lambda i, *_: (i, 0, 0)),
            scratch_shapes=[
                pltpu.VMEM((nb, width, 2 * HEAD_SIZE), jnp.bfloat16),
                pltpu.VMEM((BLK, width), jnp.float32),
            ],
        )
        outs.append(pl.pallas_call(
            functools.partial(slash_kernel, parity=parity),
            grid_spec=grid_spec,
            out_shape=jax.ShapeDtypeStruct((halves, BLK, HEAD_SIZE), jnp.bfloat16),
            compiler_params=pltpu.CompilerParams(dimension_semantics=("arbitrary",)),
        )(crow, splane, srow, pick, q4, ckv, skv, sbias4, acc4, top4, total4))
    return outs


def per_device(queries, keys, values, cache_keys, cache_values, vertical, vertical_count, slash):
    key_rows, value_rows = from_behind((keys, values), "section", 1)
    tok = queries.shape[1]
    nx = lax.axis_size("gx")
    nz = lax.axis_size("gz")
    heads = nx * nz
    kv_heads = key_rows.shape[2] // HEAD_SIZE
    prefill_stretch = tok * heads
    q_rows = queries[0].reshape(tok, heads, HEAD_SIZE)
    head_rows = lax.all_to_all(q_rows, ("gx", "gz"), split_axis=1, concat_axis=0, tiled=True)
    own_query = from_behind(head_rows.reshape(prefill_stretch, HEAD_SIZE), "section", 1)

    kv_rows = jnp.concatenate(
        [
            key_rows[0].reshape(tok, kv_heads, HEAD_SIZE),
            value_rows[0].reshape(tok, kv_heads, HEAD_SIZE),
        ],
        axis=2,
    )
    part = lax.all_to_all(kv_rows, "gx", split_axis=1, concat_axis=0, tiled=True)
    skv = lax.all_gather(part.reshape(nx * tok, 2 * HEAD_SIZE), "gz", axis=0, tiled=False)
    cache_part = jnp.concatenate([cache_keys[0, 0], cache_values[0, 0]], axis=1)
    ckv = lax.all_gather(cache_part, "gz", axis=0, tiled=True)
    halves = head_attention(own_query, ckv, skv, vertical[0, 0], vertical_count[0, 0],
                            slash[0, 0], tok)
    pieces = []
    for half in halves:
        moved = lax.all_to_all(half[:, :, None, :], ("gx", "gz"), split_axis=0, concat_axis=2,
                               tiled=True)
        pieces.append(moved.reshape(tok // 2, heads * HEAD_SIZE))
    return jnp.concatenate(pieces, axis=0).reshape(1, tok, heads * HEAD_SIZE)


def solution(mesh):
    nsec, nseq = mesh.devices.shape
    kv_groups = nseq // GROUP
    grid_mesh = Mesh(mesh.devices.reshape(nsec, kv_groups, GROUP), ("section", "gx", "gz"))
    seq = ("gx", "gz")
    return jax.shard_map(
        per_device,
        mesh=grid_mesh,
        in_specs=(
            P("section", seq, None),
            P("section", seq, None),
            P("section", seq, None),
            P("section", seq, None, None),
            P("section", seq, None, None),
            P("section", seq, None),
            P("section", seq),
            P("section", seq, None),
        ),
        out_specs=P("section", seq, None),
        check_vma=False,
    )
```

```python
import functools
import math

import jax
import jax.numpy as jnp
from jax import lax
from jax.experimental import pallas as pl
from jax.experimental.pallas import tpu as pltpu
from jax.sharding import Mesh
from jax.sharding import PartitionSpec as P

HEAD_SIZE = 128
GROUP = 8
BLK = 64
NVMAX = 32
NS = 11
CACHE = 4096
TQ = 256

big_negative = -1e30


def from_behind(x, axis, by):
    peers = lax.axis_size(axis)
    return lax.ppermute(x, axis, [(i, (i + by) % peers) for i in range(peers)])


def vertical_kernel(verts_ref, q_ref, ckv_ref, vbias_ref, acc_ref, top_ref, total_ref, kvert):
    tile = pl.program_id(0)
    softmax_scale = 1.0 / math.sqrt(HEAD_SIZE)
    ncb = CACHE // BLK

    @pl.when(tile == 0)
    def _():
        def fill(s, carry):
            blk = jnp.clip(verts_ref[s], 0, ncb - 1)
            src = pl.multiple_of(blk * BLK, BLK)
            dst = pl.multiple_of(s * BLK, BLK)
            kvert[pl.ds(dst, BLK), :] = ckv_ref[pl.ds(src, BLK), :]
            return carry

        lax.fori_loop(0, NVMAX, fill, 0)

    scores = lax.dot_general(q_ref[...], kvert[:, :HEAD_SIZE], (((1,), (1,)), ((), ())),
                             preferred_element_type=jnp.float32) * softmax_scale + vbias_ref[...]
    top = jnp.max(scores, axis=1, keepdims=True)
    weights = jnp.exp(scores - top)
    total_ref[...] = jnp.sum(weights, axis=1, keepdims=True)
    top_ref[...] = top
    acc_ref[...] = jnp.dot(weights.astype(jnp.bfloat16), kvert[:, HEAD_SIZE:],
                           preferred_element_type=jnp.float32)


def slash_kernel(crow_ref, splane_ref, srow_ref, pick_ref, q_ref, ckv_ref, skv_ref, sbias_ref,
                 acc_ref, top_ref, total_ref, o_ref, kslash, causal_bias, *, parity):
    nb = TQ // BLK
    nd = NS + 1
    width = nd * BLK
    tile = pl.program_id(0)
    softmax_scale = 1.0 / math.sqrt(HEAD_SIZE)

    @pl.when(tile == 0)
    def _():
        col = lax.broadcasted_iota(jnp.int32, (BLK, width), 1)
        row = lax.broadcasted_iota(jnp.int32, (BLK, width), 0)
        causal = (col >= BLK) | (col <= row)
        causal_bias[...] = jnp.where(causal, 0.0, big_negative).astype(jnp.float32)

    for b in range(nb):
        qb = 2 * (tile * nb + b) + parity
        for d in range(nd):
            at = qb * nd + d
            from_cache = ckv_ref[pl.ds(pl.multiple_of(crow_ref[at], BLK), BLK), :]
            from_stretch = skv_ref[splane_ref[at], pl.ds(pl.multiple_of(srow_ref[at], BLK), BLK), :]
            kslash[b, pl.ds(d * BLK, BLK), :] = jnp.where(pick_ref[at] > 0, from_stretch,
                                                          from_cache)

    q3 = q_ref[...].reshape(nb, BLK, HEAD_SIZE)
    s_s = lax.dot_general(q3, kslash[:, :, :HEAD_SIZE], (((2,), (2,)), ((0,), (0,))),
                          preferred_element_type=jnp.float32) * softmax_scale
    s_s = s_s + sbias_ref[...].reshape(nb, 1, width) + causal_bias[...][None, :, :]
    top_v = top_ref[...].reshape(nb, BLK, 1)
    top = jnp.maximum(top_v, jnp.max(s_s, axis=2, keepdims=True))
    factor = jnp.exp(top_v - top)
    p_s = jnp.exp(s_s - top)
    total = total_ref[...].reshape(nb, BLK, 1) * factor + jnp.sum(p_s, axis=2, keepdims=True)
    acc_s = lax.dot_general(p_s.astype(jnp.bfloat16), kslash[:, :, HEAD_SIZE:],
                            (((2,), (1,)), ((0,), (0,))), preferred_element_type=jnp.float32)
    acc = acc_ref[...].reshape(nb, BLK, HEAD_SIZE) * factor + acc_s
    o_ref[...] = (acc / total).astype(o_ref.dtype)


def vertical_part(own_query, ckv, verts, count):
    prefill_stretch = own_query.shape[0]
    nvc = NVMAX * BLK
    slot = jnp.arange(nvc, dtype=jnp.int32) // BLK
    vbias = jnp.where(slot < count, 0.0, big_negative).astype(jnp.float32).reshape(1, nvc)
    grid_spec = pltpu.PrefetchScalarGridSpec(
        num_scalar_prefetch=1,
        grid=(prefill_stretch // TQ,),
        in_specs=[
            pl.BlockSpec((TQ, HEAD_SIZE), lambda i, *_: (i, 0)),
            pl.BlockSpec(ckv.shape, lambda i, *_: (0, 0)),
            pl.BlockSpec((1, nvc), lambda i, *_: (0, 0)),
        ],
        out_specs=[
            pl.BlockSpec((TQ, HEAD_SIZE), lambda i, *_: (i, 0)),
            pl.BlockSpec((TQ, 1), lambda i, *_: (i, 0)),
            pl.BlockSpec((TQ, 1), lambda i, *_: (i, 0)),
        ],
        scratch_shapes=[pltpu.VMEM((nvc, 2 * HEAD_SIZE), jnp.bfloat16)],
    )
    return pl.pallas_call(
        vertical_kernel,
        grid_spec=grid_spec,
        out_shape=[
            jax.ShapeDtypeStruct((prefill_stretch, HEAD_SIZE), jnp.float32),
            jax.ShapeDtypeStruct((prefill_stretch, 1), jnp.float32),
            jax.ShapeDtypeStruct((prefill_stretch, 1), jnp.float32),
        ],
        compiler_params=pltpu.CompilerParams(dimension_semantics=("arbitrary",)),
    )(verts, own_query, ckv, vbias)


def head_attention(own_query, ckv, skv, verts, count, slashes, tok):
    prefill_stretch = own_query.shape[0]
    nz = skv.shape[0]
    ncb = CACHE // BLK
    nqb = prefill_stretch // BLK
    nd = NS + 1
    acc_v, top_v, total_v = vertical_part(own_query, ckv, verts, count)
    offsets = jnp.concatenate([jnp.zeros((1,), jnp.int32), slashes])
    blocks = ncb + jnp.arange(nqb, dtype=jnp.int32)[:, None] - offsets[None, :]
    used = jnp.arange(NVMAX, dtype=jnp.int32)[None, None, :] < count
    listed = jnp.any((blocks[:, :, None] == verts[None, None, :]) & used, axis=2)
    valid = (blocks >= 0) & jnp.logical_not(listed)
    per_dev = tok // BLK
    stretch_blk = jnp.clip(blocks - ncb, 0, nqb - 1)
    dev = stretch_blk // per_dev
    pick = (blocks >= ncb).astype(jnp.int32).reshape(-1)
    crow = (jnp.clip(blocks, 0, ncb - 1) * BLK).reshape(-1)
    splane = (dev % nz).reshape(-1)
    srow = ((dev // nz) * tok + (stretch_blk % per_dev) * BLK).reshape(-1)
    sbias = jnp.repeat(jnp.where(valid, 0.0, big_negative).astype(jnp.float32), BLK,
                       axis=1).reshape(nqb, 1, nd * BLK)
    nb = TQ // BLK
    width = nd * BLK
    halves = nqb // 2
    q4 = own_query.reshape(halves, 2, BLK, HEAD_SIZE)
    acc4 = acc_v.reshape(halves, 2, BLK, HEAD_SIZE)
    top4 = top_v.reshape(halves, 2, BLK, 1)
    total4 = total_v.reshape(halves, 2, BLK, 1)
    sbias4 = sbias.reshape(halves, 2, 1, width)
    outs = []
    for parity in range(2):
        grid_spec = pltpu.PrefetchScalarGridSpec(
            num_scalar_prefetch=4,
            grid=(halves // nb,),
            in_specs=[
                pl.BlockSpec((nb, 1, BLK, HEAD_SIZE), lambda i, *_, p=parity: (i, p, 0, 0)),
                pl.BlockSpec(ckv.shape, lambda i, *_: (0, 0)),
                pl.BlockSpec(skv.shape, lambda i, *_: (0, 0, 0)),
                pl.BlockSpec((nb, 1, 1, width), lambda i, *_, p=parity: (i, p, 0, 0)),
                pl.BlockSpec((nb, 1, BLK, HEAD_SIZE), lambda i, *_, p=parity: (i, p, 0, 0)),
                pl.BlockSpec((nb, 1, BLK, 1), lambda i, *_, p=parity: (i, p, 0, 0)),
                pl.BlockSpec((nb, 1, BLK, 1), lambda i, *_, p=parity: (i, p, 0, 0)),
            ],
            out_specs=pl.BlockSpec((nb, BLK, HEAD_SIZE), lambda i, *_: (i, 0, 0)),
            scratch_shapes=[
                pltpu.VMEM((nb, width, 2 * HEAD_SIZE), jnp.bfloat16),
                pltpu.VMEM((BLK, width), jnp.float32),
            ],
        )
        outs.append(pl.pallas_call(
            functools.partial(slash_kernel, parity=parity),
            grid_spec=grid_spec,
            out_shape=jax.ShapeDtypeStruct((halves, BLK, HEAD_SIZE), jnp.bfloat16),
            compiler_params=pltpu.CompilerParams(dimension_semantics=("arbitrary",)),
        )(crow, splane, srow, pick, q4, ckv, skv, sbias4, acc4, top4, total4))
    return outs


def per_device(queries, keys, values, cache_keys, cache_values, vertical, vertical_count, slash):
    key_rows, value_rows = from_behind((keys, values), "section", 1)
    tok = queries.shape[1]
    nx = lax.axis_size("gx")
    nz = lax.axis_size("gz")
    heads = nx * nz
    kv_heads = key_rows.shape[2] // HEAD_SIZE
    prefill_stretch = tok * heads
    q_rows = queries[0].reshape(tok, heads, HEAD_SIZE)
    head_rows = lax.all_to_all(q_rows, ("gx", "gz"), split_axis=1, concat_axis=0, tiled=True)
    own_query = from_behind(head_rows.reshape(prefill_stretch, HEAD_SIZE), "section", 1)

    kv_rows = jnp.concatenate(
        [
            key_rows[0].reshape(tok, kv_heads, HEAD_SIZE),
            value_rows[0].reshape(tok, kv_heads, HEAD_SIZE),
        ],
        axis=2,
    )
    part = lax.all_to_all(kv_rows, "gx", split_axis=1, concat_axis=0, tiled=True)
    skv = lax.all_gather(part.reshape(nx * tok, 2 * HEAD_SIZE), "gz", axis=0, tiled=False)
    cache_part = jnp.concatenate([cache_keys[0, 0], cache_values[0, 0]], axis=1)
    copies = jnp.broadcast_to(cache_part[None], (nz,) + cache_part.shape)
    ckv = lax.all_to_all(copies, "gz", split_axis=0, concat_axis=0, tiled=True).reshape(
        nz * cache_part.shape[0], 2 * HEAD_SIZE)
    halves = head_attention(own_query, ckv, skv, vertical[0, 0], vertical_count[0, 0],
                            slash[0, 0], tok)
    pieces = []
    for half in halves:
        moved = lax.all_to_all(half[:, :, None, :], ("gx", "gz"), split_axis=0, concat_axis=2,
                               tiled=True)
        pieces.append(moved.reshape(tok // 2, heads * HEAD_SIZE))
    return jnp.concatenate(pieces, axis=0).reshape(1, tok, heads * HEAD_SIZE)


def solution(mesh):
    nsec, nseq = mesh.devices.shape
    kv_groups = nseq // GROUP
    grid_mesh = Mesh(mesh.devices.reshape(nsec, kv_groups, GROUP), ("section", "gx", "gz"))
    seq = ("gx", "gz")
    return jax.shard_map(
        per_device,
        mesh=grid_mesh,
        in_specs=(
            P("section", seq, None),
            P("section", seq, None),
            P("section", seq, None),
            P("section", seq, None, None),
            P("section", seq, None, None),
            P("section", seq, None),
            P("section", seq),
            P("section", seq, None),
        ),
        out_specs=P("section", seq, None),
        check_vma=False,
    )
```

```python
import functools
import math

import jax
import jax.numpy as jnp
from jax import lax
from jax.experimental import pallas as pl
from jax.experimental.pallas import tpu as pltpu
from jax.sharding import Mesh
from jax.sharding import PartitionSpec as P

HEAD_SIZE = 128
GROUP = 8
BLK = 64
NVMAX = 32
NS = 11
CACHE = 4096
TQ = 256
STQ = 512

big_negative = -1e30


def from_behind(x, axis, by):
    peers = lax.axis_size(axis)
    return lax.ppermute(x, axis, [(i, (i + by) % peers) for i in range(peers)])


def vertical_kernel(verts_ref, q_ref, ckv_ref, vbias_ref, acc_ref, top_ref, total_ref, kvert):
    tile = pl.program_id(0)
    softmax_scale = 1.0 / math.sqrt(HEAD_SIZE)
    ncb = CACHE // BLK

    @pl.when(tile == 0)
    def _():
        def fill(s, carry):
            blk = jnp.clip(verts_ref[s], 0, ncb - 1)
            src = pl.multiple_of(blk * BLK, BLK)
            dst = pl.multiple_of(s * BLK, BLK)
            kvert[pl.ds(dst, BLK), :] = ckv_ref[pl.ds(src, BLK), :]
            return carry

        lax.fori_loop(0, NVMAX, fill, 0)

    scores = lax.dot_general(q_ref[...], kvert[:, :HEAD_SIZE], (((1,), (1,)), ((), ())),
                             preferred_element_type=jnp.float32) * softmax_scale + vbias_ref[...]
    top = jnp.max(scores, axis=1, keepdims=True)
    weights = jnp.exp(scores - top)
    total_ref[...] = jnp.sum(weights, axis=1, keepdims=True)
    top_ref[...] = top
    acc_ref[...] = jnp.dot(weights.astype(jnp.bfloat16), kvert[:, HEAD_SIZE:],
                           preferred_element_type=jnp.float32)


def slash_kernel(crow_ref, splane_ref, srow_ref, pick_ref, q_ref, ckv_ref, skv_ref, sbias_ref,
                 acc_ref, top_ref, total_ref, o_ref, kslash, causal_bias, *, parity):
    nb = STQ // BLK
    nd = NS + 1
    width = nd * BLK
    tile = pl.program_id(0)
    softmax_scale = 1.0 / math.sqrt(HEAD_SIZE)

    @pl.when(tile == 0)
    def _():
        col = lax.broadcasted_iota(jnp.int32, (BLK, width), 1)
        row = lax.broadcasted_iota(jnp.int32, (BLK, width), 0)
        causal = (col >= BLK) | (col <= row)
        causal_bias[...] = jnp.where(causal, 0.0, big_negative).astype(jnp.float32)

    for b in range(nb):
        qb = 2 * (tile * nb + b) + parity
        for d in range(nd):
            at = qb * nd + d
            from_cache = ckv_ref[pl.ds(pl.multiple_of(crow_ref[at], BLK), BLK), :]
            from_stretch = skv_ref[splane_ref[at], pl.ds(pl.multiple_of(srow_ref[at], BLK), BLK), :]
            kslash[b, pl.ds(d * BLK, BLK), :] = jnp.where(pick_ref[at] > 0, from_stretch,
                                                          from_cache)

    q3 = q_ref[...].reshape(nb, BLK, HEAD_SIZE)
    s_s = lax.dot_general(q3, kslash[:, :, :HEAD_SIZE], (((2,), (2,)), ((0,), (0,))),
                          preferred_element_type=jnp.float32) * softmax_scale
    s_s = s_s + sbias_ref[...].reshape(nb, 1, width) + causal_bias[...][None, :, :]
    top_v = top_ref[...].reshape(nb, BLK, 1)
    top = jnp.maximum(top_v, jnp.max(s_s, axis=2, keepdims=True))
    factor = jnp.exp(top_v - top)
    p_s = jnp.exp(s_s - top)
    total = total_ref[...].reshape(nb, BLK, 1) * factor + jnp.sum(p_s, axis=2, keepdims=True)
    acc_s = lax.dot_general(p_s.astype(jnp.bfloat16), kslash[:, :, HEAD_SIZE:],
                            (((2,), (1,)), ((0,), (0,))), preferred_element_type=jnp.float32)
    acc = acc_ref[...].reshape(nb, BLK, HEAD_SIZE) * factor + acc_s
    o_ref[...] = (acc / total).astype(o_ref.dtype)


def vertical_part(own_query, ckv, verts, count):
    prefill_stretch = own_query.shape[0]
    nvc = NVMAX * BLK
    slot = jnp.arange(nvc, dtype=jnp.int32) // BLK
    vbias = jnp.where(slot < count, 0.0, big_negative).astype(jnp.float32).reshape(1, nvc)
    grid_spec = pltpu.PrefetchScalarGridSpec(
        num_scalar_prefetch=1,
        grid=(prefill_stretch // TQ,),
        in_specs=[
            pl.BlockSpec((TQ, HEAD_SIZE), lambda i, *_: (i, 0)),
            pl.BlockSpec(ckv.shape, lambda i, *_: (0, 0)),
            pl.BlockSpec((1, nvc), lambda i, *_: (0, 0)),
        ],
        out_specs=[
            pl.BlockSpec((TQ, HEAD_SIZE), lambda i, *_: (i, 0)),
            pl.BlockSpec((TQ, 1), lambda i, *_: (i, 0)),
            pl.BlockSpec((TQ, 1), lambda i, *_: (i, 0)),
        ],
        scratch_shapes=[pltpu.VMEM((nvc, 2 * HEAD_SIZE), jnp.bfloat16)],
    )
    return pl.pallas_call(
        vertical_kernel,
        grid_spec=grid_spec,
        out_shape=[
            jax.ShapeDtypeStruct((prefill_stretch, HEAD_SIZE), jnp.float32),
            jax.ShapeDtypeStruct((prefill_stretch, 1), jnp.float32),
            jax.ShapeDtypeStruct((prefill_stretch, 1), jnp.float32),
        ],
        compiler_params=pltpu.CompilerParams(dimension_semantics=("arbitrary",)),
    )(verts, own_query, ckv, vbias)


def head_attention(own_query, ckv, skv, verts, count, slashes, tok):
    prefill_stretch = own_query.shape[0]
    nz = skv.shape[0]
    ncb = CACHE // BLK
    nqb = prefill_stretch // BLK
    nd = NS + 1
    acc_v, top_v, total_v = vertical_part(own_query, ckv, verts, count)
    offsets = jnp.concatenate([jnp.zeros((1,), jnp.int32), slashes])
    blocks = ncb + jnp.arange(nqb, dtype=jnp.int32)[:, None] - offsets[None, :]
    used = jnp.arange(NVMAX, dtype=jnp.int32)[None, None, :] < count
    listed = jnp.any((blocks[:, :, None] == verts[None, None, :]) & used, axis=2)
    valid = (blocks >= 0) & jnp.logical_not(listed)
    per_dev = tok // BLK
    stretch_blk = jnp.clip(blocks - ncb, 0, nqb - 1)
    dev = stretch_blk // per_dev
    pick = (blocks >= ncb).astype(jnp.int32).reshape(-1)
    crow = (jnp.clip(blocks, 0, ncb - 1) * BLK).reshape(-1)
    splane = (dev % nz).reshape(-1)
    srow = ((dev // nz) * tok + (stretch_blk % per_dev) * BLK).reshape(-1)
    sbias = jnp.repeat(jnp.where(valid, 0.0, big_negative).astype(jnp.float32), BLK,
                       axis=1).reshape(nqb, 1, nd * BLK)
    nb = STQ // BLK
    width = nd * BLK
    halves = nqb // 2
    q4 = own_query.reshape(halves, 2, BLK, HEAD_SIZE)
    acc4 = acc_v.reshape(halves, 2, BLK, HEAD_SIZE)
    top4 = top_v.reshape(halves, 2, BLK, 1)
    total4 = total_v.reshape(halves, 2, BLK, 1)
    sbias4 = sbias.reshape(halves, 2, 1, width)
    outs = []
    for parity in range(2):
        grid_spec = pltpu.PrefetchScalarGridSpec(
            num_scalar_prefetch=4,
            grid=(halves // nb,),
            in_specs=[
                pl.BlockSpec((nb, 1, BLK, HEAD_SIZE), lambda i, *_, p=parity: (i, p, 0, 0)),
                pl.BlockSpec(ckv.shape, lambda i, *_: (0, 0)),
                pl.BlockSpec(skv.shape, lambda i, *_: (0, 0, 0)),
                pl.BlockSpec((nb, 1, 1, width), lambda i, *_, p=parity: (i, p, 0, 0)),
                pl.BlockSpec((nb, 1, BLK, HEAD_SIZE), lambda i, *_, p=parity: (i, p, 0, 0)),
                pl.BlockSpec((nb, 1, BLK, 1), lambda i, *_, p=parity: (i, p, 0, 0)),
                pl.BlockSpec((nb, 1, BLK, 1), lambda i, *_, p=parity: (i, p, 0, 0)),
            ],
            out_specs=pl.BlockSpec((nb, BLK, HEAD_SIZE), lambda i, *_: (i, 0, 0)),
            scratch_shapes=[
                pltpu.VMEM((nb, width, 2 * HEAD_SIZE), jnp.bfloat16),
                pltpu.VMEM((BLK, width), jnp.float32),
            ],
        )
        outs.append(pl.pallas_call(
            functools.partial(slash_kernel, parity=parity),
            grid_spec=grid_spec,
            out_shape=jax.ShapeDtypeStruct((halves, BLK, HEAD_SIZE), jnp.bfloat16),
            compiler_params=pltpu.CompilerParams(dimension_semantics=("arbitrary",)),
        )(crow, splane, srow, pick, q4, ckv, skv, sbias4, acc4, top4, total4))
    return outs


def per_device(queries, keys, values, cache_keys, cache_values, vertical, vertical_count, slash):
    query_rows, key_rows, value_rows = from_behind((queries, keys, values), "section", 1)
    tok = query_rows.shape[1]
    nx = lax.axis_size("gx")
    nz = lax.axis_size("gz")
    heads = nx * nz
    kv_heads = key_rows.shape[2] // HEAD_SIZE
    prefill_stretch = tok * heads
    q_rows = query_rows[0].reshape(tok, heads, HEAD_SIZE)
    own_query = lax.all_to_all(
        q_rows, ("gx", "gz"), split_axis=1, concat_axis=0, tiled=True
    ).reshape(prefill_stretch, HEAD_SIZE)

    kv_rows = jnp.concatenate(
        [
            key_rows[0].reshape(tok, kv_heads, HEAD_SIZE),
            value_rows[0].reshape(tok, kv_heads, HEAD_SIZE),
        ],
        axis=2,
    )
    part = lax.all_to_all(kv_rows, "gx", split_axis=1, concat_axis=0, tiled=True)
    skv = lax.all_gather(part.reshape(nx * tok, 2 * HEAD_SIZE), "gz", axis=0, tiled=False)
    cache_part = jnp.concatenate([cache_keys[0, 0], cache_values[0, 0]], axis=1)
    ckv = lax.all_gather(cache_part, "gz", axis=0, tiled=True)
    halves = head_attention(own_query, ckv, skv, vertical[0, 0], vertical_count[0, 0],
                            slash[0, 0], tok)
    pieces = []
    for half in halves:
        moved = lax.all_to_all(half[:, :, None, :], ("gx", "gz"), split_axis=0, concat_axis=2,
                               tiled=True)
        pieces.append(moved.reshape(tok // 2, heads * HEAD_SIZE))
    return jnp.concatenate(pieces, axis=0).reshape(1, tok, heads * HEAD_SIZE)


def solution(mesh):
    nsec, nseq = mesh.devices.shape
    kv_groups = nseq // GROUP
    grid_mesh = Mesh(mesh.devices.reshape(nsec, kv_groups, GROUP), ("section", "gx", "gz"))
    seq = ("gx", "gz")
    return jax.shard_map(
        per_device,
        mesh=grid_mesh,
        in_specs=(
            P("section", seq, None),
            P("section", seq, None),
            P("section", seq, None),
            P("section", seq, None, None),
            P("section", seq, None, None),
            P("section", seq, None),
            P("section", seq),
            P("section", seq, None),
        ),
        out_specs=P("section", seq, None),
        check_vma=False,
    )
```

```python
import functools
import math

import jax
import jax.numpy as jnp
from jax import lax
from jax.experimental import pallas as pl
from jax.experimental.pallas import tpu as pltpu
from jax.sharding import Mesh
from jax.sharding import PartitionSpec as P

HEAD_SIZE = 128
GROUP = 8
BLK = 64
NVMAX = 32
NS = 11
CACHE = 4096
TQ = 256
STQ = 1024

big_negative = -1e30


def from_behind(x, axis, by):
    peers = lax.axis_size(axis)
    return lax.ppermute(x, axis, [(i, (i + by) % peers) for i in range(peers)])


def vertical_kernel(verts_ref, q_ref, ckv_ref, vbias_ref, acc_ref, top_ref, total_ref, kvert):
    tile = pl.program_id(0)
    softmax_scale = 1.0 / math.sqrt(HEAD_SIZE)
    ncb = CACHE // BLK

    @pl.when(tile == 0)
    def _():
        def fill(s, carry):
            blk = jnp.clip(verts_ref[s], 0, ncb - 1)
            src = pl.multiple_of(blk * BLK, BLK)
            dst = pl.multiple_of(s * BLK, BLK)
            kvert[pl.ds(dst, BLK), :] = ckv_ref[pl.ds(src, BLK), :]
            return carry

        lax.fori_loop(0, NVMAX, fill, 0)

    scores = lax.dot_general(q_ref[...], kvert[:, :HEAD_SIZE], (((1,), (1,)), ((), ())),
                             preferred_element_type=jnp.float32) * softmax_scale + vbias_ref[...]
    top = jnp.max(scores, axis=1, keepdims=True)
    weights = jnp.exp(scores - top)
    total_ref[...] = jnp.sum(weights, axis=1, keepdims=True)
    top_ref[...] = top
    acc_ref[...] = jnp.dot(weights.astype(jnp.bfloat16), kvert[:, HEAD_SIZE:],
                           preferred_element_type=jnp.float32)


def slash_kernel(crow_ref, splane_ref, srow_ref, pick_ref, q_ref, ckv_ref, skv_ref, sbias_ref,
                 acc_ref, top_ref, total_ref, o_ref, kslash, causal_bias, *, parity):
    nb = STQ // BLK
    nd = NS + 1
    width = nd * BLK
    tile = pl.program_id(0)
    softmax_scale = 1.0 / math.sqrt(HEAD_SIZE)

    @pl.when(tile == 0)
    def _():
        col = lax.broadcasted_iota(jnp.int32, (BLK, width), 1)
        row = lax.broadcasted_iota(jnp.int32, (BLK, width), 0)
        causal = (col >= BLK) | (col <= row)
        causal_bias[...] = jnp.where(causal, 0.0, big_negative).astype(jnp.float32)

    for b in range(nb):
        qb = 2 * (tile * nb + b) + parity
        for d in range(nd):
            at = qb * nd + d
            from_cache = ckv_ref[pl.ds(pl.multiple_of(crow_ref[at], BLK), BLK), :]
            from_stretch = skv_ref[splane_ref[at], pl.ds(pl.multiple_of(srow_ref[at], BLK), BLK), :]
            kslash[b, pl.ds(d * BLK, BLK), :] = jnp.where(pick_ref[at] > 0, from_stretch,
                                                          from_cache)

    q3 = q_ref[...].reshape(nb, BLK, HEAD_SIZE)
    s_s = lax.dot_general(q3, kslash[:, :, :HEAD_SIZE], (((2,), (2,)), ((0,), (0,))),
                          preferred_element_type=jnp.float32) * softmax_scale
    s_s = s_s + sbias_ref[...].reshape(nb, 1, width) + causal_bias[...][None, :, :]
    top_v = top_ref[...].reshape(nb, BLK, 1)
    top = jnp.maximum(top_v, jnp.max(s_s, axis=2, keepdims=True))
    factor = jnp.exp(top_v - top)
    p_s = jnp.exp(s_s - top)
    total = total_ref[...].reshape(nb, BLK, 1) * factor + jnp.sum(p_s, axis=2, keepdims=True)
    acc_s = lax.dot_general(p_s.astype(jnp.bfloat16), kslash[:, :, HEAD_SIZE:],
                            (((2,), (1,)), ((0,), (0,))), preferred_element_type=jnp.float32)
    acc = acc_ref[...].reshape(nb, BLK, HEAD_SIZE) * factor + acc_s
    o_ref[...] = (acc / total).astype(o_ref.dtype)


def vertical_part(own_query, ckv, verts, count):
    prefill_stretch = own_query.shape[0]
    nvc = NVMAX * BLK
    slot = jnp.arange(nvc, dtype=jnp.int32) // BLK
    vbias = jnp.where(slot < count, 0.0, big_negative).astype(jnp.float32).reshape(1, nvc)
    grid_spec = pltpu.PrefetchScalarGridSpec(
        num_scalar_prefetch=1,
        grid=(prefill_stretch // TQ,),
        in_specs=[
            pl.BlockSpec((TQ, HEAD_SIZE), lambda i, *_: (i, 0)),
            pl.BlockSpec(ckv.shape, lambda i, *_: (0, 0)),
            pl.BlockSpec((1, nvc), lambda i, *_: (0, 0)),
        ],
        out_specs=[
            pl.BlockSpec((TQ, HEAD_SIZE), lambda i, *_: (i, 0)),
            pl.BlockSpec((TQ, 1), lambda i, *_: (i, 0)),
            pl.BlockSpec((TQ, 1), lambda i, *_: (i, 0)),
        ],
        scratch_shapes=[pltpu.VMEM((nvc, 2 * HEAD_SIZE), jnp.bfloat16)],
    )
    return pl.pallas_call(
        vertical_kernel,
        grid_spec=grid_spec,
        out_shape=[
            jax.ShapeDtypeStruct((prefill_stretch, HEAD_SIZE), jnp.float32),
            jax.ShapeDtypeStruct((prefill_stretch, 1), jnp.float32),
            jax.ShapeDtypeStruct((prefill_stretch, 1), jnp.float32),
        ],
        compiler_params=pltpu.CompilerParams(dimension_semantics=("arbitrary",)),
    )(verts, own_query, ckv, vbias)


def head_attention(own_query, ckv, skv, verts, count, slashes, tok):
    prefill_stretch = own_query.shape[0]
    nz = skv.shape[0]
    ncb = CACHE // BLK
    nqb = prefill_stretch // BLK
    nd = NS + 1
    acc_v, top_v, total_v = vertical_part(own_query, ckv, verts, count)
    offsets = jnp.concatenate([jnp.zeros((1,), jnp.int32), slashes])
    blocks = ncb + jnp.arange(nqb, dtype=jnp.int32)[:, None] - offsets[None, :]
    used = jnp.arange(NVMAX, dtype=jnp.int32)[None, None, :] < count
    listed = jnp.any((blocks[:, :, None] == verts[None, None, :]) & used, axis=2)
    valid = (blocks >= 0) & jnp.logical_not(listed)
    per_dev = tok // BLK
    stretch_blk = jnp.clip(blocks - ncb, 0, nqb - 1)
    dev = stretch_blk // per_dev
    pick = (blocks >= ncb).astype(jnp.int32).reshape(-1)
    crow = (jnp.clip(blocks, 0, ncb - 1) * BLK).reshape(-1)
    splane = (dev % nz).reshape(-1)
    srow = ((dev // nz) * tok + (stretch_blk % per_dev) * BLK).reshape(-1)
    sbias = jnp.repeat(jnp.where(valid, 0.0, big_negative).astype(jnp.float32), BLK,
                       axis=1).reshape(nqb, 1, nd * BLK)
    nb = STQ // BLK
    width = nd * BLK
    halves = nqb // 2
    q4 = own_query.reshape(halves, 2, BLK, HEAD_SIZE)
    acc4 = acc_v.reshape(halves, 2, BLK, HEAD_SIZE)
    top4 = top_v.reshape(halves, 2, BLK, 1)
    total4 = total_v.reshape(halves, 2, BLK, 1)
    sbias4 = sbias.reshape(halves, 2, 1, width)
    outs = []
    for parity in range(2):
        grid_spec = pltpu.PrefetchScalarGridSpec(
            num_scalar_prefetch=4,
            grid=(halves // nb,),
            in_specs=[
                pl.BlockSpec((nb, 1, BLK, HEAD_SIZE), lambda i, *_, p=parity: (i, p, 0, 0)),
                pl.BlockSpec(ckv.shape, lambda i, *_: (0, 0)),
                pl.BlockSpec(skv.shape, lambda i, *_: (0, 0, 0)),
                pl.BlockSpec((nb, 1, 1, width), lambda i, *_, p=parity: (i, p, 0, 0)),
                pl.BlockSpec((nb, 1, BLK, HEAD_SIZE), lambda i, *_, p=parity: (i, p, 0, 0)),
                pl.BlockSpec((nb, 1, BLK, 1), lambda i, *_, p=parity: (i, p, 0, 0)),
                pl.BlockSpec((nb, 1, BLK, 1), lambda i, *_, p=parity: (i, p, 0, 0)),
            ],
            out_specs=pl.BlockSpec((nb, BLK, HEAD_SIZE), lambda i, *_: (i, 0, 0)),
            scratch_shapes=[
                pltpu.VMEM((nb, width, 2 * HEAD_SIZE), jnp.bfloat16),
                pltpu.VMEM((BLK, width), jnp.float32),
            ],
        )
        outs.append(pl.pallas_call(
            functools.partial(slash_kernel, parity=parity),
            grid_spec=grid_spec,
            out_shape=jax.ShapeDtypeStruct((halves, BLK, HEAD_SIZE), jnp.bfloat16),
            compiler_params=pltpu.CompilerParams(dimension_semantics=("arbitrary",)),
        )(crow, splane, srow, pick, q4, ckv, skv, sbias4, acc4, top4, total4))
    return outs


def per_device(queries, keys, values, cache_keys, cache_values, vertical, vertical_count, slash):
    query_rows, key_rows, value_rows = from_behind((queries, keys, values), "section", 1)
    tok = query_rows.shape[1]
    nx = lax.axis_size("gx")
    nz = lax.axis_size("gz")
    heads = nx * nz
    kv_heads = key_rows.shape[2] // HEAD_SIZE
    prefill_stretch = tok * heads
    q_rows = query_rows[0].reshape(tok, heads, HEAD_SIZE)
    own_query = lax.all_to_all(
        q_rows, ("gx", "gz"), split_axis=1, concat_axis=0, tiled=True
    ).reshape(prefill_stretch, HEAD_SIZE)

    kv_rows = jnp.concatenate(
        [
            key_rows[0].reshape(tok, kv_heads, HEAD_SIZE),
            value_rows[0].reshape(tok, kv_heads, HEAD_SIZE),
        ],
        axis=2,
    )
    part = lax.all_to_all(kv_rows, "gx", split_axis=1, concat_axis=0, tiled=True)
    skv = lax.all_gather(part.reshape(nx * tok, 2 * HEAD_SIZE), "gz", axis=0, tiled=False)
    cache_part = jnp.concatenate([cache_keys[0, 0], cache_values[0, 0]], axis=1)
    ckv = lax.all_gather(cache_part, "gz", axis=0, tiled=True)
    halves = head_attention(own_query, ckv, skv, vertical[0, 0], vertical_count[0, 0],
                            slash[0, 0], tok)
    pieces = []
    for half in halves:
        moved = lax.all_to_all(half[:, :, None, :], ("gx", "gz"), split_axis=0, concat_axis=2,
                               tiled=True)
        pieces.append(moved.reshape(tok // 2, heads * HEAD_SIZE))
    return jnp.concatenate(pieces, axis=0).reshape(1, tok, heads * HEAD_SIZE)


def solution(mesh):
    nsec, nseq = mesh.devices.shape
    kv_groups = nseq // GROUP
    grid_mesh = Mesh(mesh.devices.reshape(nsec, kv_groups, GROUP), ("section", "gx", "gz"))
    seq = ("gx", "gz")
    return jax.shard_map(
        per_device,
        mesh=grid_mesh,
        in_specs=(
            P("section", seq, None),
            P("section", seq, None),
            P("section", seq, None),
            P("section", seq, None, None),
            P("section", seq, None, None),
            P("section", seq, None),
            P("section", seq),
            P("section", seq, None),
        ),
        out_specs=P("section", seq, None),
        check_vma=False,
    )
```

```python
import functools
import math

import jax
import jax.numpy as jnp
from jax import lax
from jax.experimental import pallas as pl
from jax.experimental.pallas import tpu as pltpu
from jax.sharding import Mesh
from jax.sharding import PartitionSpec as P

HEAD_SIZE = 128
GROUP = 8
BLK = 64
NVMAX = 32
NS = 11
CACHE = 4096
TQ = 256
STQ = 512

big_negative = -1e30


def from_behind(x, axis, by):
    peers = lax.axis_size(axis)
    return lax.ppermute(x, axis, [(i, (i + by) % peers) for i in range(peers)])


def vertical_kernel(verts_ref, q_ref, kv_ref, vbias_ref, acc_ref, top_ref, total_ref, kvert):
    tile = pl.program_id(0)
    softmax_scale = 1.0 / math.sqrt(HEAD_SIZE)
    ncb = CACHE // BLK

    @pl.when(tile == 0)
    def _():
        def fill(s, carry):
            blk = jnp.clip(verts_ref[s], 0, ncb - 1)
            per = kv_ref.shape[1] // BLK
            src = pl.multiple_of((blk % per) * BLK, BLK)
            dst = pl.multiple_of(s * BLK, BLK)
            kvert[pl.ds(dst, BLK), :] = kv_ref[blk // per, pl.ds(src, BLK), pl.ds(0, 2 * HEAD_SIZE)]
            return carry

        lax.fori_loop(0, NVMAX, fill, 0)

    scores = lax.dot_general(q_ref[...], kvert[:, :HEAD_SIZE], (((1,), (1,)), ((), ())),
                             preferred_element_type=jnp.float32) * softmax_scale + vbias_ref[...]
    top = jnp.max(scores, axis=1, keepdims=True)
    weights = jnp.exp(scores - top)
    total_ref[...] = jnp.sum(weights, axis=1, keepdims=True)
    top_ref[...] = top
    acc_ref[...] = jnp.dot(weights.astype(jnp.bfloat16), kvert[:, HEAD_SIZE:],
                           preferred_element_type=jnp.float32)


def slash_kernel(cplane_ref, crow_ref, splane_ref, srow_ref, pick_ref, q_ref, kv_ref, sbias_ref,
                 acc_ref, top_ref, total_ref, o_ref, kslash, causal_bias, *, parity):
    nb = STQ // BLK
    nd = NS + 1
    width = nd * BLK
    tile = pl.program_id(0)
    softmax_scale = 1.0 / math.sqrt(HEAD_SIZE)

    @pl.when(tile == 0)
    def _():
        col = lax.broadcasted_iota(jnp.int32, (BLK, width), 1)
        row = lax.broadcasted_iota(jnp.int32, (BLK, width), 0)
        causal = (col >= BLK) | (col <= row)
        causal_bias[...] = jnp.where(causal, 0.0, big_negative).astype(jnp.float32)

    for b in range(nb):
        qb = 2 * (tile * nb + b) + parity
        for d in range(nd):
            at = qb * nd + d
            from_cache = kv_ref[cplane_ref[at], pl.ds(pl.multiple_of(crow_ref[at], BLK), BLK),
                                pl.ds(0, 2 * HEAD_SIZE)]
            from_stretch = kv_ref[splane_ref[at], pl.ds(pl.multiple_of(srow_ref[at], BLK), BLK),
                                  pl.ds(2 * HEAD_SIZE, 2 * HEAD_SIZE)]
            kslash[b, pl.ds(d * BLK, BLK), :] = jnp.where(pick_ref[at] > 0, from_stretch,
                                                          from_cache)

    q3 = q_ref[...].reshape(nb, BLK, HEAD_SIZE)
    s_s = lax.dot_general(q3, kslash[:, :, :HEAD_SIZE], (((2,), (2,)), ((0,), (0,))),
                          preferred_element_type=jnp.float32) * softmax_scale
    s_s = s_s + sbias_ref[...].reshape(nb, 1, width) + causal_bias[...][None, :, :]
    top_v = top_ref[...].reshape(nb, BLK, 1)
    top = jnp.maximum(top_v, jnp.max(s_s, axis=2, keepdims=True))
    factor = jnp.exp(top_v - top)
    p_s = jnp.exp(s_s - top)
    total = total_ref[...].reshape(nb, BLK, 1) * factor + jnp.sum(p_s, axis=2, keepdims=True)
    acc_s = lax.dot_general(p_s.astype(jnp.bfloat16), kslash[:, :, HEAD_SIZE:],
                            (((2,), (1,)), ((0,), (0,))), preferred_element_type=jnp.float32)
    acc = acc_ref[...].reshape(nb, BLK, HEAD_SIZE) * factor + acc_s
    o_ref[...] = (acc / total).astype(o_ref.dtype)


def vertical_part(own_query, kv, verts, count):
    prefill_stretch = own_query.shape[0]
    nvc = NVMAX * BLK
    slot = jnp.arange(nvc, dtype=jnp.int32) // BLK
    vbias = jnp.where(slot < count, 0.0, big_negative).astype(jnp.float32).reshape(1, nvc)
    grid_spec = pltpu.PrefetchScalarGridSpec(
        num_scalar_prefetch=1,
        grid=(prefill_stretch // TQ,),
        in_specs=[
            pl.BlockSpec((TQ, HEAD_SIZE), lambda i, *_: (i, 0)),
            pl.BlockSpec(kv.shape, lambda i, *_: (0, 0, 0)),
            pl.BlockSpec((1, nvc), lambda i, *_: (0, 0)),
        ],
        out_specs=[
            pl.BlockSpec((TQ, HEAD_SIZE), lambda i, *_: (i, 0)),
            pl.BlockSpec((TQ, 1), lambda i, *_: (i, 0)),
            pl.BlockSpec((TQ, 1), lambda i, *_: (i, 0)),
        ],
        scratch_shapes=[pltpu.VMEM((nvc, 2 * HEAD_SIZE), jnp.bfloat16)],
    )
    return pl.pallas_call(
        vertical_kernel,
        grid_spec=grid_spec,
        out_shape=[
            jax.ShapeDtypeStruct((prefill_stretch, HEAD_SIZE), jnp.float32),
            jax.ShapeDtypeStruct((prefill_stretch, 1), jnp.float32),
            jax.ShapeDtypeStruct((prefill_stretch, 1), jnp.float32),
        ],
        compiler_params=pltpu.CompilerParams(dimension_semantics=("arbitrary",)),
    )(verts, own_query, kv, vbias)


def head_attention(own_query, kv, verts, count, slashes, tok):
    prefill_stretch = own_query.shape[0]
    nz = kv.shape[0]
    cache_per = kv.shape[1] // BLK
    ncb = CACHE // BLK
    nqb = prefill_stretch // BLK
    nd = NS + 1
    acc_v, top_v, total_v = vertical_part(own_query, kv, verts, count)
    offsets = jnp.concatenate([jnp.zeros((1,), jnp.int32), slashes])
    blocks = ncb + jnp.arange(nqb, dtype=jnp.int32)[:, None] - offsets[None, :]
    used = jnp.arange(NVMAX, dtype=jnp.int32)[None, None, :] < count
    listed = jnp.any((blocks[:, :, None] == verts[None, None, :]) & used, axis=2)
    valid = (blocks >= 0) & jnp.logical_not(listed)
    per_dev = tok // BLK
    stretch_blk = jnp.clip(blocks - ncb, 0, nqb - 1)
    dev = stretch_blk // per_dev
    pick = (blocks >= ncb).astype(jnp.int32).reshape(-1)
    cache_blk = jnp.clip(blocks, 0, ncb - 1)
    cplane = (cache_blk // cache_per).reshape(-1)
    crow = ((cache_blk % cache_per) * BLK).reshape(-1)
    splane = (dev % nz).reshape(-1)
    srow = ((dev // nz) * tok + (stretch_blk % per_dev) * BLK).reshape(-1)
    sbias = jnp.repeat(jnp.where(valid, 0.0, big_negative).astype(jnp.float32), BLK,
                       axis=1).reshape(nqb, 1, nd * BLK)
    nb = STQ // BLK
    width = nd * BLK
    halves = nqb // 2
    q4 = own_query.reshape(halves, 2, BLK, HEAD_SIZE)
    acc4 = acc_v.reshape(halves, 2, BLK, HEAD_SIZE)
    top4 = top_v.reshape(halves, 2, BLK, 1)
    total4 = total_v.reshape(halves, 2, BLK, 1)
    sbias4 = sbias.reshape(halves, 2, 1, width)
    outs = []
    for parity in range(2):
        grid_spec = pltpu.PrefetchScalarGridSpec(
            num_scalar_prefetch=5,
            grid=(halves // nb,),
            in_specs=[
                pl.BlockSpec((nb, 1, BLK, HEAD_SIZE), lambda i, *_, p=parity: (i, p, 0, 0)),
                pl.BlockSpec(kv.shape, lambda i, *_: (0, 0, 0)),
                pl.BlockSpec((nb, 1, 1, width), lambda i, *_, p=parity: (i, p, 0, 0)),
                pl.BlockSpec((nb, 1, BLK, HEAD_SIZE), lambda i, *_, p=parity: (i, p, 0, 0)),
                pl.BlockSpec((nb, 1, BLK, 1), lambda i, *_, p=parity: (i, p, 0, 0)),
                pl.BlockSpec((nb, 1, BLK, 1), lambda i, *_, p=parity: (i, p, 0, 0)),
            ],
            out_specs=pl.BlockSpec((nb, BLK, HEAD_SIZE), lambda i, *_: (i, 0, 0)),
            scratch_shapes=[
                pltpu.VMEM((nb, width, 2 * HEAD_SIZE), jnp.bfloat16),
                pltpu.VMEM((BLK, width), jnp.float32),
            ],
        )
        outs.append(pl.pallas_call(
            functools.partial(slash_kernel, parity=parity),
            grid_spec=grid_spec,
            out_shape=jax.ShapeDtypeStruct((halves, BLK, HEAD_SIZE), jnp.bfloat16),
            compiler_params=pltpu.CompilerParams(dimension_semantics=("arbitrary",)),
        )(cplane, crow, splane, srow, pick, q4, kv, sbias4, acc4, top4, total4))
    return outs


def per_device(queries, keys, values, cache_keys, cache_values, vertical, vertical_count, slash):
    query_rows, key_rows, value_rows = from_behind((queries, keys, values), "section", 1)
    tok = query_rows.shape[1]
    nx = lax.axis_size("gx")
    nz = lax.axis_size("gz")
    heads = nx * nz
    kv_heads = key_rows.shape[2] // HEAD_SIZE
    prefill_stretch = tok * heads
    q_rows = query_rows[0].reshape(tok, heads, HEAD_SIZE)
    own_query = lax.all_to_all(
        q_rows, ("gx", "gz"), split_axis=1, concat_axis=0, tiled=True
    ).reshape(prefill_stretch, HEAD_SIZE)

    kv_rows = jnp.concatenate(
        [
            key_rows[0].reshape(tok, kv_heads, HEAD_SIZE),
            value_rows[0].reshape(tok, kv_heads, HEAD_SIZE),
        ],
        axis=2,
    )
    part = lax.all_to_all(kv_rows, "gx", split_axis=1, concat_axis=0, tiled=True)
    shard = jnp.concatenate(
        [cache_keys[0, 0], cache_values[0, 0], part.reshape(nx * tok, 2 * HEAD_SIZE)], axis=1)
    kv = lax.all_gather(shard, "gz", axis=0, tiled=False)
    halves = head_attention(own_query, kv, vertical[0, 0], vertical_count[0, 0], slash[0, 0],
                            tok)
    pieces = []
    for half in halves:
        moved = lax.all_to_all(half[:, :, None, :], ("gx", "gz"), split_axis=0, concat_axis=2,
                               tiled=True)
        pieces.append(moved.reshape(tok // 2, heads * HEAD_SIZE))
    return jnp.concatenate(pieces, axis=0).reshape(1, tok, heads * HEAD_SIZE)


def solution(mesh):
    nsec, nseq = mesh.devices.shape
    kv_groups = nseq // GROUP
    grid_mesh = Mesh(mesh.devices.reshape(nsec, kv_groups, GROUP), ("section", "gx", "gz"))
    seq = ("gx", "gz")
    return jax.shard_map(
        per_device,
        mesh=grid_mesh,
        in_specs=(
            P("section", seq, None),
            P("section", seq, None),
            P("section", seq, None),
            P("section", seq, None, None),
            P("section", seq, None, None),
            P("section", seq, None),
            P("section", seq),
            P("section", seq, None),
        ),
        out_specs=P("section", seq, None),
        check_vma=False,
    )
```

```python
import functools
import math

import jax
import jax.numpy as jnp
from jax import lax
from jax.experimental import pallas as pl
from jax.experimental.pallas import tpu as pltpu
from jax.sharding import Mesh
from jax.sharding import PartitionSpec as P

HEAD_SIZE = 128
GROUP = 8
BLK = 64
NVMAX = 32
NS = 11
CACHE = 4096
TQ = 256
STQ = 512

big_negative = -1e30


def from_behind(x, axis, by):
    peers = lax.axis_size(axis)
    return lax.ppermute(x, axis, [(i, (i + by) % peers) for i in range(peers)])


def vertical_kernel(verts_ref, q_ref, ckv_ref, vbias_ref, acc_ref, top_ref, total_ref, kvert):
    tile = pl.program_id(0)
    softmax_scale = 1.0 / math.sqrt(HEAD_SIZE)
    ncb = CACHE // BLK

    @pl.when(tile == 0)
    def _():
        def fill(s, carry):
            blk = jnp.clip(verts_ref[s], 0, ncb - 1)
            src = pl.multiple_of(blk * BLK, BLK)
            dst = pl.multiple_of(s * BLK, BLK)
            kvert[pl.ds(dst, BLK), :] = ckv_ref[pl.ds(src, BLK), :]
            return carry

        lax.fori_loop(0, NVMAX, fill, 0)

    scores = lax.dot_general(q_ref[...], kvert[:, :HEAD_SIZE], (((1,), (1,)), ((), ())),
                             preferred_element_type=jnp.float32) * softmax_scale + vbias_ref[...]
    top = jnp.max(scores, axis=1, keepdims=True)
    weights = jnp.exp(scores - top)
    total_ref[...] = jnp.sum(weights, axis=1, keepdims=True)
    top_ref[...] = top
    acc_ref[...] = jnp.dot(weights.astype(jnp.bfloat16), kvert[:, HEAD_SIZE:],
                           preferred_element_type=jnp.float32)


def slash_kernel(urow_ref, q_ref, ckv_hbm, skv_hbm, sbias_ref, acc_ref, top_ref, total_ref,
                 o_ref, kslash, causal_bias, kvall, sems, *, parity):
    nb = STQ // BLK
    nd = NS + 1
    width = nd * BLK
    tile = pl.program_id(0)
    softmax_scale = 1.0 / math.sqrt(HEAD_SIZE)

    @pl.when(tile == 0)
    def _():
        col = lax.broadcasted_iota(jnp.int32, (BLK, width), 1)
        row = lax.broadcasted_iota(jnp.int32, (BLK, width), 0)
        causal = (col >= BLK) | (col <= row)
        causal_bias[...] = jnp.where(causal, 0.0, big_negative).astype(jnp.float32)
        cache_rows = ckv_hbm.shape[0]
        first = pltpu.make_async_copy(ckv_hbm, kvall.at[pl.ds(0, cache_rows)], sems.at[0])
        second = pltpu.make_async_copy(skv_hbm, kvall.at[pl.ds(cache_rows, skv_hbm.shape[0])],
                                       sems.at[1])
        first.start()
        second.start()
        first.wait()
        second.wait()

    for b in range(nb):
        qb = 2 * (tile * nb + b) + parity
        for d in range(nd):
            at = qb * nd + d
            kslash[b, pl.ds(d * BLK, BLK), :] = kvall[pl.ds(pl.multiple_of(urow_ref[at], BLK),
                                                             BLK), :]

    q3 = q_ref[...].reshape(nb, BLK, HEAD_SIZE)
    s_s = lax.dot_general(q3, kslash[:, :, :HEAD_SIZE], (((2,), (2,)), ((0,), (0,))),
                          preferred_element_type=jnp.float32) * softmax_scale
    s_s = s_s + sbias_ref[...].reshape(nb, 1, width) + causal_bias[...][None, :, :]
    top_v = top_ref[...].reshape(nb, BLK, 1)
    top = jnp.maximum(top_v, jnp.max(s_s, axis=2, keepdims=True))
    factor = jnp.exp(top_v - top)
    p_s = jnp.exp(s_s - top)
    total = total_ref[...].reshape(nb, BLK, 1) * factor + jnp.sum(p_s, axis=2, keepdims=True)
    acc_s = lax.dot_general(p_s.astype(jnp.bfloat16), kslash[:, :, HEAD_SIZE:],
                            (((2,), (1,)), ((0,), (0,))), preferred_element_type=jnp.float32)
    acc = acc_ref[...].reshape(nb, BLK, HEAD_SIZE) * factor + acc_s
    o_ref[...] = (acc / total).astype(o_ref.dtype)


def vertical_part(own_query, ckv, verts, count):
    prefill_stretch = own_query.shape[0]
    nvc = NVMAX * BLK
    slot = jnp.arange(nvc, dtype=jnp.int32) // BLK
    vbias = jnp.where(slot < count, 0.0, big_negative).astype(jnp.float32).reshape(1, nvc)
    grid_spec = pltpu.PrefetchScalarGridSpec(
        num_scalar_prefetch=1,
        grid=(prefill_stretch // TQ,),
        in_specs=[
            pl.BlockSpec((TQ, HEAD_SIZE), lambda i, *_: (i, 0)),
            pl.BlockSpec(ckv.shape, lambda i, *_: (0, 0)),
            pl.BlockSpec((1, nvc), lambda i, *_: (0, 0)),
        ],
        out_specs=[
            pl.BlockSpec((TQ, HEAD_SIZE), lambda i, *_: (i, 0)),
            pl.BlockSpec((TQ, 1), lambda i, *_: (i, 0)),
            pl.BlockSpec((TQ, 1), lambda i, *_: (i, 0)),
        ],
        scratch_shapes=[pltpu.VMEM((nvc, 2 * HEAD_SIZE), jnp.bfloat16)],
    )
    return pl.pallas_call(
        vertical_kernel,
        grid_spec=grid_spec,
        out_shape=[
            jax.ShapeDtypeStruct((prefill_stretch, HEAD_SIZE), jnp.float32),
            jax.ShapeDtypeStruct((prefill_stretch, 1), jnp.float32),
            jax.ShapeDtypeStruct((prefill_stretch, 1), jnp.float32),
        ],
        compiler_params=pltpu.CompilerParams(dimension_semantics=("arbitrary",)),
    )(verts, own_query, ckv, vbias)


def head_attention(own_query, ckv, skv, verts, count, slashes, tok):
    prefill_stretch = own_query.shape[0]
    nz = skv.shape[0]
    ncb = CACHE // BLK
    nqb = prefill_stretch // BLK
    nd = NS + 1
    acc_v, top_v, total_v = vertical_part(own_query, ckv, verts, count)
    offsets = jnp.concatenate([jnp.zeros((1,), jnp.int32), slashes])
    blocks = ncb + jnp.arange(nqb, dtype=jnp.int32)[:, None] - offsets[None, :]
    used = jnp.arange(NVMAX, dtype=jnp.int32)[None, None, :] < count
    listed = jnp.any((blocks[:, :, None] == verts[None, None, :]) & used, axis=2)
    valid = (blocks >= 0) & jnp.logical_not(listed)
    per_dev = tok // BLK
    stretch_blk = jnp.clip(blocks - ncb, 0, nqb - 1)
    dev = stretch_blk // per_dev
    cache_rows = ckv.shape[0]
    part_rows = skv.shape[1]
    srow = cache_rows + (dev % nz) * part_rows + (dev // nz) * tok + (stretch_blk % per_dev) * BLK
    urow = jnp.where(blocks >= ncb, srow, jnp.clip(blocks, 0, ncb - 1) * BLK).reshape(-1)
    flat_skv = skv.reshape(nz * part_rows, 2 * HEAD_SIZE)
    sbias = jnp.repeat(jnp.where(valid, 0.0, big_negative).astype(jnp.float32), BLK,
                       axis=1).reshape(nqb, 1, nd * BLK)
    nb = STQ // BLK
    width = nd * BLK
    halves = nqb // 2
    q4 = own_query.reshape(halves, 2, BLK, HEAD_SIZE)
    acc4 = acc_v.reshape(halves, 2, BLK, HEAD_SIZE)
    top4 = top_v.reshape(halves, 2, BLK, 1)
    total4 = total_v.reshape(halves, 2, BLK, 1)
    sbias4 = sbias.reshape(halves, 2, 1, width)
    outs = []
    for parity in range(2):
        grid_spec = pltpu.PrefetchScalarGridSpec(
            num_scalar_prefetch=1,
            grid=(halves // nb,),
            in_specs=[
                pl.BlockSpec((nb, 1, BLK, HEAD_SIZE), lambda i, *_, p=parity: (i, p, 0, 0)),
                pl.BlockSpec(memory_space=pl.ANY),
                pl.BlockSpec(memory_space=pl.ANY),
                pl.BlockSpec((nb, 1, 1, width), lambda i, *_, p=parity: (i, p, 0, 0)),
                pl.BlockSpec((nb, 1, BLK, HEAD_SIZE), lambda i, *_, p=parity: (i, p, 0, 0)),
                pl.BlockSpec((nb, 1, BLK, 1), lambda i, *_, p=parity: (i, p, 0, 0)),
                pl.BlockSpec((nb, 1, BLK, 1), lambda i, *_, p=parity: (i, p, 0, 0)),
            ],
            out_specs=pl.BlockSpec((nb, BLK, HEAD_SIZE), lambda i, *_: (i, 0, 0)),
            scratch_shapes=[
                pltpu.VMEM((nb, width, 2 * HEAD_SIZE), jnp.bfloat16),
                pltpu.VMEM((BLK, width), jnp.float32),
                pltpu.VMEM((ckv.shape[0] + nz * part_rows, 2 * HEAD_SIZE), jnp.bfloat16),
                pltpu.SemaphoreType.DMA((2,)),
            ],
        )
        outs.append(pl.pallas_call(
            functools.partial(slash_kernel, parity=parity),
            grid_spec=grid_spec,
            out_shape=jax.ShapeDtypeStruct((halves, BLK, HEAD_SIZE), jnp.bfloat16),
            compiler_params=pltpu.CompilerParams(dimension_semantics=("arbitrary",)),
        )(urow, q4, ckv, flat_skv, sbias4, acc4, top4, total4))
    return outs


def per_device(queries, keys, values, cache_keys, cache_values, vertical, vertical_count, slash):
    query_rows, key_rows, value_rows = from_behind((queries, keys, values), "section", 1)
    tok = query_rows.shape[1]
    nx = lax.axis_size("gx")
    nz = lax.axis_size("gz")
    heads = nx * nz
    kv_heads = key_rows.shape[2] // HEAD_SIZE
    prefill_stretch = tok * heads
    q_rows = query_rows[0].reshape(tok, heads, HEAD_SIZE)
    own_query = lax.all_to_all(
        q_rows, ("gx", "gz"), split_axis=1, concat_axis=0, tiled=True
    ).reshape(prefill_stretch, HEAD_SIZE)

    kv_rows = jnp.concatenate(
        [
            key_rows[0].reshape(tok, kv_heads, HEAD_SIZE),
            value_rows[0].reshape(tok, kv_heads, HEAD_SIZE),
        ],
        axis=2,
    )
    part = lax.all_to_all(kv_rows, "gx", split_axis=1, concat_axis=0, tiled=True)
    skv = lax.all_gather(part.reshape(nx * tok, 2 * HEAD_SIZE), "gz", axis=0, tiled=False)
    cache_part = jnp.concatenate([cache_keys[0, 0], cache_values[0, 0]], axis=1)
    ckv = lax.all_gather(cache_part, "gz", axis=0, tiled=True)
    halves = head_attention(own_query, ckv, skv, vertical[0, 0], vertical_count[0, 0],
                            slash[0, 0], tok)
    pieces = []
    for half in halves:
        moved = lax.all_to_all(half[:, :, None, :], ("gx", "gz"), split_axis=0, concat_axis=2,
                               tiled=True)
        pieces.append(moved.reshape(tok // 2, heads * HEAD_SIZE))
    return jnp.concatenate(pieces, axis=0).reshape(1, tok, heads * HEAD_SIZE)


def solution(mesh):
    nsec, nseq = mesh.devices.shape
    kv_groups = nseq // GROUP
    grid_mesh = Mesh(mesh.devices.reshape(nsec, kv_groups, GROUP), ("section", "gx", "gz"))
    seq = ("gx", "gz")
    return jax.shard_map(
        per_device,
        mesh=grid_mesh,
        in_specs=(
            P("section", seq, None),
            P("section", seq, None),
            P("section", seq, None),
            P("section", seq, None, None),
            P("section", seq, None, None),
            P("section", seq, None),
            P("section", seq),
            P("section", seq, None),
        ),
        out_specs=P("section", seq, None),
        check_vma=False,
    )
```

```python
import functools
import math

import jax
import jax.numpy as jnp
from jax import lax
from jax.experimental import pallas as pl
from jax.experimental.pallas import tpu as pltpu
from jax.sharding import Mesh
from jax.sharding import PartitionSpec as P

HEAD_SIZE = 128
GROUP = 8
BLK = 64
NVMAX = 32
NS = 11
CACHE = 4096
TQ = 256
STQ = 512

big_negative = -1e30


def from_behind(x, axis, by):
    peers = lax.axis_size(axis)
    return lax.ppermute(x, axis, [(i, (i + by) % peers) for i in range(peers)])


def vertical_kernel(verts_ref, q_ref, ckv_ref, vbias_ref, acc_ref, top_ref, total_ref, kvert):
    tile = pl.program_id(0)
    softmax_scale = 1.0 / math.sqrt(HEAD_SIZE)
    ncb = CACHE // BLK

    @pl.when(tile == 0)
    def _():
        def fill(s, carry):
            blk = jnp.clip(verts_ref[s], 0, ncb - 1)
            src = pl.multiple_of(blk * BLK, BLK)
            dst = pl.multiple_of(s * BLK, BLK)
            kvert[pl.ds(dst, BLK), :] = ckv_ref[pl.ds(src, BLK), :]
            return carry

        lax.fori_loop(0, NVMAX, fill, 0)

    scores = lax.dot_general(q_ref[...], kvert[:, :HEAD_SIZE], (((1,), (1,)), ((), ())),
                             preferred_element_type=jnp.float32) * softmax_scale + vbias_ref[...]
    top = jnp.max(scores, axis=1, keepdims=True)
    weights = jnp.exp(scores - top)
    total_ref[...] = jnp.sum(weights, axis=1, keepdims=True)
    top_ref[...] = top
    acc_ref[...] = jnp.dot(weights.astype(jnp.bfloat16), kvert[:, HEAD_SIZE:],
                           preferred_element_type=jnp.float32)


def slash_kernel(crow_ref, splane_ref, srow_ref, pick_ref, q_ref, ckv_ref, skv_ref, sbias_ref,
                 acc_ref, top_ref, total_ref, o_ref, kslash, causal_bias, *, parity):
    nb = STQ // BLK
    nd = NS + 1
    width = nd * BLK
    tile = pl.program_id(0)
    softmax_scale = 1.0 / math.sqrt(HEAD_SIZE)

    @pl.when(tile == 0)
    def _():
        col = lax.broadcasted_iota(jnp.int32, (BLK, width), 1)
        row = lax.broadcasted_iota(jnp.int32, (BLK, width), 0)
        causal = (col >= BLK) | (col <= row)
        causal_bias[...] = jnp.where(causal, 0.0, big_negative).astype(jnp.float32)

    for b in range(nb):
        qb = 2 * (tile * nb + b) + parity
        for d in range(nd):
            at = qb * nd + d
            from_cache = ckv_ref[pl.ds(pl.multiple_of(crow_ref[at], BLK), BLK), :]
            from_stretch = skv_ref[splane_ref[at], pl.ds(pl.multiple_of(srow_ref[at], BLK), BLK), :]
            kslash[b, pl.ds(d * BLK, BLK), :] = jnp.where(pick_ref[at] > 0, from_stretch,
                                                          from_cache)

    q3 = q_ref[...].reshape(nb, BLK, HEAD_SIZE)
    s_s = lax.dot_general(q3, kslash[:, :, :HEAD_SIZE], (((2,), (2,)), ((0,), (0,))),
                          preferred_element_type=jnp.float32) * softmax_scale
    s_s = s_s + sbias_ref[...].reshape(nb, 1, width) + causal_bias[...][None, :, :]
    top_v = top_ref[...].reshape(nb, BLK, 1)
    top = jnp.maximum(top_v, jnp.max(s_s, axis=2, keepdims=True))
    factor = jnp.exp(top_v - top)
    p_s = jnp.exp(s_s - top)
    total = total_ref[...].reshape(nb, BLK, 1) * factor + jnp.sum(p_s, axis=2, keepdims=True)
    acc_s = lax.dot_general(p_s.astype(jnp.bfloat16), kslash[:, :, HEAD_SIZE:],
                            (((2,), (1,)), ((0,), (0,))), preferred_element_type=jnp.float32)
    acc = acc_ref[...].reshape(nb, BLK, HEAD_SIZE) * factor + acc_s
    o_ref[...] = (acc / total).astype(o_ref.dtype)


def vertical_part(own_query, ckv, verts, count):
    prefill_stretch = own_query.shape[0]
    nvc = NVMAX * BLK
    slot = jnp.arange(nvc, dtype=jnp.int32) // BLK
    vbias = jnp.where(slot < count, 0.0, big_negative).astype(jnp.float32).reshape(1, nvc)
    grid_spec = pltpu.PrefetchScalarGridSpec(
        num_scalar_prefetch=1,
        grid=(prefill_stretch // TQ,),
        in_specs=[
            pl.BlockSpec((TQ, HEAD_SIZE), lambda i, *_: (i, 0)),
            pl.BlockSpec(ckv.shape, lambda i, *_: (0, 0)),
            pl.BlockSpec((1, nvc), lambda i, *_: (0, 0)),
        ],
        out_specs=[
            pl.BlockSpec((TQ, HEAD_SIZE), lambda i, *_: (i, 0)),
            pl.BlockSpec((TQ, 1), lambda i, *_: (i, 0)),
            pl.BlockSpec((TQ, 1), lambda i, *_: (i, 0)),
        ],
        scratch_shapes=[pltpu.VMEM((nvc, 2 * HEAD_SIZE), jnp.bfloat16)],
    )
    return pl.pallas_call(
        vertical_kernel,
        grid_spec=grid_spec,
        out_shape=[
            jax.ShapeDtypeStruct((prefill_stretch, HEAD_SIZE), jnp.float32),
            jax.ShapeDtypeStruct((prefill_stretch, 1), jnp.float32),
            jax.ShapeDtypeStruct((prefill_stretch, 1), jnp.float32),
        ],
        compiler_params=pltpu.CompilerParams(dimension_semantics=("arbitrary",)),
    )(verts, own_query, ckv, vbias)


def head_attention(own_query, ckv, skv, verts, count, slashes, tok):
    prefill_stretch = own_query.shape[0]
    nz = skv.shape[0]
    ncb = CACHE // BLK
    nqb = prefill_stretch // BLK
    nd = NS + 1
    acc_v, top_v, total_v = vertical_part(own_query, ckv, verts, count)
    offsets = jnp.concatenate([jnp.zeros((1,), jnp.int32), slashes])
    blocks = ncb + jnp.arange(nqb, dtype=jnp.int32)[:, None] - offsets[None, :]
    used = jnp.arange(NVMAX, dtype=jnp.int32)[None, None, :] < count
    listed = jnp.any((blocks[:, :, None] == verts[None, None, :]) & used, axis=2)
    valid = (blocks >= 0) & jnp.logical_not(listed)
    per_dev = tok // BLK
    stretch_blk = jnp.clip(blocks - ncb, 0, nqb - 1)
    dev = stretch_blk // per_dev
    pick = (blocks >= ncb).astype(jnp.int32).reshape(-1)
    crow = (jnp.clip(blocks, 0, ncb - 1) * BLK).reshape(-1)
    splane = (dev % nz).reshape(-1)
    srow = ((dev // nz) * tok + (stretch_blk % per_dev) * BLK).reshape(-1)
    sbias = jnp.repeat(jnp.where(valid, 0.0, big_negative).astype(jnp.float32), BLK,
                       axis=1).reshape(nqb, 1, nd * BLK)
    nb = STQ // BLK
    width = nd * BLK
    halves = nqb // 2
    q4 = own_query.reshape(halves, 2, BLK, HEAD_SIZE)
    acc4 = acc_v.reshape(halves, 2, BLK, HEAD_SIZE)
    top4 = top_v.reshape(halves, 2, BLK, 1)
    total4 = total_v.reshape(halves, 2, BLK, 1)
    sbias4 = sbias.reshape(halves, 2, 1, width)
    outs = []
    for parity in range(2):
        grid_spec = pltpu.PrefetchScalarGridSpec(
            num_scalar_prefetch=4,
            grid=(halves // nb,),
            in_specs=[
                pl.BlockSpec((nb, 1, BLK, HEAD_SIZE), lambda i, *_, p=parity: (i, p, 0, 0)),
                pl.BlockSpec(ckv.shape, lambda i, *_: (0, 0)),
                pl.BlockSpec(skv.shape, lambda i, *_: (0, 0, 0)),
                pl.BlockSpec((nb, 1, 1, width), lambda i, *_, p=parity: (i, p, 0, 0)),
                pl.BlockSpec((nb, 1, BLK, HEAD_SIZE), lambda i, *_, p=parity: (i, p, 0, 0)),
                pl.BlockSpec((nb, 1, BLK, 1), lambda i, *_, p=parity: (i, p, 0, 0)),
                pl.BlockSpec((nb, 1, BLK, 1), lambda i, *_, p=parity: (i, p, 0, 0)),
            ],
            out_specs=pl.BlockSpec((nb, BLK, HEAD_SIZE), lambda i, *_: (i, 0, 0)),
            scratch_shapes=[
                pltpu.VMEM((nb, width, 2 * HEAD_SIZE), jnp.bfloat16),
                pltpu.VMEM((BLK, width), jnp.float32),
            ],
        )
        outs.append(pl.pallas_call(
            functools.partial(slash_kernel, parity=parity),
            grid_spec=grid_spec,
            out_shape=jax.ShapeDtypeStruct((halves, BLK, HEAD_SIZE), jnp.bfloat16),
            compiler_params=pltpu.CompilerParams(dimension_semantics=("arbitrary",)),
        )(crow, splane, srow, pick, q4, ckv, skv, sbias4, acc4, top4, total4))
    return outs


def per_device(queries, keys, values, cache_keys, cache_values, vertical, vertical_count, slash):
    query_rows, key_rows, value_rows = from_behind((queries, keys, values), "section", 1)
    tok = query_rows.shape[1]
    nx = lax.axis_size("gx")
    nz = lax.axis_size("gz")
    heads = nx * nz
    kv_heads = key_rows.shape[2] // HEAD_SIZE
    prefill_stretch = tok * heads
    q_rows = query_rows[0].reshape(tok, heads, HEAD_SIZE)
    own_query = lax.all_to_all(
        q_rows, ("gx", "gz"), split_axis=1, concat_axis=0, tiled=True
    ).reshape(prefill_stretch, HEAD_SIZE)

    kv_rows = jnp.concatenate(
        [
            key_rows[0].reshape(tok, kv_heads, HEAD_SIZE),
            value_rows[0].reshape(tok, kv_heads, HEAD_SIZE),
        ],
        axis=2,
    )
    part = lax.all_to_all(kv_rows, "gx", split_axis=1, concat_axis=0, tiled=True)
    skv = lax.all_gather(part.reshape(nx * tok, 2 * HEAD_SIZE), "gz", axis=0, tiled=False)
    cache_part = jnp.concatenate([cache_keys[0, 0], cache_values[0, 0]], axis=1)
    ckv = lax.all_gather(cache_part, "gz", axis=0, tiled=True)
    halves = head_attention(own_query, ckv, skv, vertical[0, 0], vertical_count[0, 0],
                            slash[0, 0], tok)
    pieces = []
    for half in halves:
        moved = lax.all_to_all(half, ("gx", "gz"), split_axis=0, concat_axis=0, tiled=True)
        pieces.append(moved.transpose(1, 0, 2).reshape(tok // 2, heads * HEAD_SIZE))
    return jnp.concatenate(pieces, axis=0).reshape(1, tok, heads * HEAD_SIZE)


def solution(mesh):
    nsec, nseq = mesh.devices.shape
    kv_groups = nseq // GROUP
    grid_mesh = Mesh(mesh.devices.reshape(nsec, kv_groups, GROUP), ("section", "gx", "gz"))
    seq = ("gx", "gz")
    return jax.shard_map(
        per_device,
        mesh=grid_mesh,
        in_specs=(
            P("section", seq, None),
            P("section", seq, None),
            P("section", seq, None),
            P("section", seq, None, None),
            P("section", seq, None, None),
            P("section", seq, None),
            P("section", seq),
            P("section", seq, None),
        ),
        out_specs=P("section", seq, None),
        check_vma=False,
    )
```

```python
import functools
import math

import jax
import jax.numpy as jnp
from jax import lax
from jax.experimental import pallas as pl
from jax.experimental.pallas import tpu as pltpu
from jax.sharding import Mesh
from jax.sharding import PartitionSpec as P

HEAD_SIZE = 128
GROUP = 8
BLK = 64
NVMAX = 32
NS = 11
CACHE = 4096
TQ = 256
STQ = 512

big_negative = -1e30


def from_behind(x, axis, by):
    peers = lax.axis_size(axis)
    return lax.ppermute(x, axis, [(i, (i + by) % peers) for i in range(peers)])


def vertical_kernel(verts_ref, q_ref, ckv_ref, vbias_ref, acc_ref, top_ref, total_ref, kvert):
    tile = pl.program_id(0)
    softmax_scale = 1.0 / math.sqrt(HEAD_SIZE)
    ncb = CACHE // BLK

    @pl.when(tile == 0)
    def _():
        def fill(s, carry):
            blk = jnp.clip(verts_ref[s], 0, ncb - 1)
            half = ckv_ref.shape[1] // 2
            per = half // BLK
            src = pl.multiple_of((blk % per) * BLK, BLK)
            dst = pl.multiple_of(s * BLK, BLK)
            kvert[pl.ds(dst, BLK), pl.ds(0, HEAD_SIZE)] = ckv_ref[blk // per, pl.ds(src, BLK), :]
            kvert[pl.ds(dst, BLK), pl.ds(HEAD_SIZE, HEAD_SIZE)] = ckv_ref[
                blk // per, pl.ds(src + half, BLK), :]
            return carry

        lax.fori_loop(0, NVMAX, fill, 0)

    scores = lax.dot_general(q_ref[...], kvert[:, :HEAD_SIZE], (((1,), (1,)), ((), ())),
                             preferred_element_type=jnp.float32) * softmax_scale + vbias_ref[...]
    top = jnp.max(scores, axis=1, keepdims=True)
    weights = jnp.exp(scores - top)
    total_ref[...] = jnp.sum(weights, axis=1, keepdims=True)
    top_ref[...] = top
    acc_ref[...] = jnp.dot(weights.astype(jnp.bfloat16), kvert[:, HEAD_SIZE:],
                           preferred_element_type=jnp.float32)


def slash_kernel(cplane_ref, crow_ref, splane_ref, srow_ref, pick_ref, q_ref, ckv_ref, skv_ref,
                 sbias_ref,
                 acc_ref, top_ref, total_ref, o_ref, kslash, causal_bias, *, parity):
    nb = STQ // BLK
    nd = NS + 1
    width = nd * BLK
    tile = pl.program_id(0)
    softmax_scale = 1.0 / math.sqrt(HEAD_SIZE)

    @pl.when(tile == 0)
    def _():
        col = lax.broadcasted_iota(jnp.int32, (BLK, width), 1)
        row = lax.broadcasted_iota(jnp.int32, (BLK, width), 0)
        causal = (col >= BLK) | (col <= row)
        causal_bias[...] = jnp.where(causal, 0.0, big_negative).astype(jnp.float32)

    for b in range(nb):
        qb = 2 * (tile * nb + b) + parity
        for d in range(nd):
            at = qb * nd + d
            half = ckv_ref.shape[1] // 2
            crow = pl.multiple_of(crow_ref[at], BLK)
            cplane = cplane_ref[at]
            take = pick_ref[at] > 0
            from_stretch = skv_ref[splane_ref[at], pl.ds(pl.multiple_of(srow_ref[at], BLK), BLK), :]
            kslash[b, pl.ds(d * BLK, BLK), pl.ds(0, HEAD_SIZE)] = jnp.where(
                take, from_stretch[:, :HEAD_SIZE], ckv_ref[cplane, pl.ds(crow, BLK), :])
            kslash[b, pl.ds(d * BLK, BLK), pl.ds(HEAD_SIZE, HEAD_SIZE)] = jnp.where(
                take, from_stretch[:, HEAD_SIZE:], ckv_ref[cplane, pl.ds(crow + half, BLK), :])

    q3 = q_ref[...].reshape(nb, BLK, HEAD_SIZE)
    s_s = lax.dot_general(q3, kslash[:, :, :HEAD_SIZE], (((2,), (2,)), ((0,), (0,))),
                          preferred_element_type=jnp.float32) * softmax_scale
    s_s = s_s + sbias_ref[...].reshape(nb, 1, width) + causal_bias[...][None, :, :]
    top_v = top_ref[...].reshape(nb, BLK, 1)
    top = jnp.maximum(top_v, jnp.max(s_s, axis=2, keepdims=True))
    factor = jnp.exp(top_v - top)
    p_s = jnp.exp(s_s - top)
    total = total_ref[...].reshape(nb, BLK, 1) * factor + jnp.sum(p_s, axis=2, keepdims=True)
    acc_s = lax.dot_general(p_s.astype(jnp.bfloat16), kslash[:, :, HEAD_SIZE:],
                            (((2,), (1,)), ((0,), (0,))), preferred_element_type=jnp.float32)
    acc = acc_ref[...].reshape(nb, BLK, HEAD_SIZE) * factor + acc_s
    o_ref[...] = (acc / total).astype(o_ref.dtype)


def vertical_part(own_query, ckv, verts, count):
    prefill_stretch = own_query.shape[0]
    nvc = NVMAX * BLK
    slot = jnp.arange(nvc, dtype=jnp.int32) // BLK
    vbias = jnp.where(slot < count, 0.0, big_negative).astype(jnp.float32).reshape(1, nvc)
    grid_spec = pltpu.PrefetchScalarGridSpec(
        num_scalar_prefetch=1,
        grid=(prefill_stretch // TQ,),
        in_specs=[
            pl.BlockSpec((TQ, HEAD_SIZE), lambda i, *_: (i, 0)),
            pl.BlockSpec(ckv.shape, lambda i, *_: (0, 0, 0)),
            pl.BlockSpec((1, nvc), lambda i, *_: (0, 0)),
        ],
        out_specs=[
            pl.BlockSpec((TQ, HEAD_SIZE), lambda i, *_: (i, 0)),
            pl.BlockSpec((TQ, 1), lambda i, *_: (i, 0)),
            pl.BlockSpec((TQ, 1), lambda i, *_: (i, 0)),
        ],
        scratch_shapes=[pltpu.VMEM((nvc, 2 * HEAD_SIZE), jnp.bfloat16)],
    )
    return pl.pallas_call(
        vertical_kernel,
        grid_spec=grid_spec,
        out_shape=[
            jax.ShapeDtypeStruct((prefill_stretch, HEAD_SIZE), jnp.float32),
            jax.ShapeDtypeStruct((prefill_stretch, 1), jnp.float32),
            jax.ShapeDtypeStruct((prefill_stretch, 1), jnp.float32),
        ],
        compiler_params=pltpu.CompilerParams(dimension_semantics=("arbitrary",)),
    )(verts, own_query, ckv, vbias)


def head_attention(own_query, ckv, skv, verts, count, slashes, tok):
    prefill_stretch = own_query.shape[0]
    nz = skv.shape[0]
    ncb = CACHE // BLK
    nqb = prefill_stretch // BLK
    nd = NS + 1
    acc_v, top_v, total_v = vertical_part(own_query, ckv, verts, count)
    offsets = jnp.concatenate([jnp.zeros((1,), jnp.int32), slashes])
    blocks = ncb + jnp.arange(nqb, dtype=jnp.int32)[:, None] - offsets[None, :]
    used = jnp.arange(NVMAX, dtype=jnp.int32)[None, None, :] < count
    listed = jnp.any((blocks[:, :, None] == verts[None, None, :]) & used, axis=2)
    valid = (blocks >= 0) & jnp.logical_not(listed)
    per_dev = tok // BLK
    stretch_blk = jnp.clip(blocks - ncb, 0, nqb - 1)
    dev = stretch_blk // per_dev
    pick = (blocks >= ncb).astype(jnp.int32).reshape(-1)
    cache_per = ckv.shape[1] // 2 // BLK
    cache_blk = jnp.clip(blocks, 0, ncb - 1)
    cplane = (cache_blk // cache_per).reshape(-1)
    crow = ((cache_blk % cache_per) * BLK).reshape(-1)
    splane = (dev % nz).reshape(-1)
    srow = ((dev // nz) * tok + (stretch_blk % per_dev) * BLK).reshape(-1)
    sbias = jnp.repeat(jnp.where(valid, 0.0, big_negative).astype(jnp.float32), BLK,
                       axis=1).reshape(nqb, 1, nd * BLK)
    nb = STQ // BLK
    width = nd * BLK
    halves = nqb // 2
    q4 = own_query.reshape(halves, 2, BLK, HEAD_SIZE)
    acc4 = acc_v.reshape(halves, 2, BLK, HEAD_SIZE)
    top4 = top_v.reshape(halves, 2, BLK, 1)
    total4 = total_v.reshape(halves, 2, BLK, 1)
    sbias4 = sbias.reshape(halves, 2, 1, width)
    outs = []
    for parity in range(2):
        grid_spec = pltpu.PrefetchScalarGridSpec(
            num_scalar_prefetch=5,
            grid=(halves // nb,),
            in_specs=[
                pl.BlockSpec((nb, 1, BLK, HEAD_SIZE), lambda i, *_, p=parity: (i, p, 0, 0)),
                pl.BlockSpec(ckv.shape, lambda i, *_: (0, 0, 0)),
                pl.BlockSpec(skv.shape, lambda i, *_: (0, 0, 0)),
                pl.BlockSpec((nb, 1, 1, width), lambda i, *_, p=parity: (i, p, 0, 0)),
                pl.BlockSpec((nb, 1, BLK, HEAD_SIZE), lambda i, *_, p=parity: (i, p, 0, 0)),
                pl.BlockSpec((nb, 1, BLK, 1), lambda i, *_, p=parity: (i, p, 0, 0)),
                pl.BlockSpec((nb, 1, BLK, 1), lambda i, *_, p=parity: (i, p, 0, 0)),
            ],
            out_specs=pl.BlockSpec((nb, BLK, HEAD_SIZE), lambda i, *_: (i, 0, 0)),
            scratch_shapes=[
                pltpu.VMEM((nb, width, 2 * HEAD_SIZE), jnp.bfloat16),
                pltpu.VMEM((BLK, width), jnp.float32),
            ],
        )
        outs.append(pl.pallas_call(
            functools.partial(slash_kernel, parity=parity),
            grid_spec=grid_spec,
            out_shape=jax.ShapeDtypeStruct((halves, BLK, HEAD_SIZE), jnp.bfloat16),
            compiler_params=pltpu.CompilerParams(dimension_semantics=("arbitrary",)),
        )(cplane, crow, splane, srow, pick, q4, ckv, skv, sbias4, acc4, top4, total4))
    return outs


def per_device(queries, keys, values, cache_keys, cache_values, vertical, vertical_count, slash):
    query_rows, key_rows, value_rows = from_behind((queries, keys, values), "section", 1)
    tok = query_rows.shape[1]
    nx = lax.axis_size("gx")
    nz = lax.axis_size("gz")
    heads = nx * nz
    kv_heads = key_rows.shape[2] // HEAD_SIZE
    prefill_stretch = tok * heads
    q_rows = query_rows[0].reshape(tok, heads, HEAD_SIZE)
    own_query = lax.all_to_all(
        q_rows, ("gx", "gz"), split_axis=1, concat_axis=0, tiled=True
    ).reshape(prefill_stretch, HEAD_SIZE)

    kv_rows = jnp.concatenate(
        [
            key_rows[0].reshape(tok, kv_heads, HEAD_SIZE),
            value_rows[0].reshape(tok, kv_heads, HEAD_SIZE),
        ],
        axis=2,
    )
    part = lax.all_to_all(kv_rows, "gx", split_axis=1, concat_axis=0, tiled=True)
    skv = lax.all_gather(part.reshape(nx * tok, 2 * HEAD_SIZE), "gz", axis=0, tiled=False)
    cache_part = jnp.concatenate([cache_keys[0, 0], cache_values[0, 0]], axis=0)
    ckv = lax.all_gather(cache_part, "gz", axis=0, tiled=False)
    halves = head_attention(own_query, ckv, skv, vertical[0, 0], vertical_count[0, 0],
                            slash[0, 0], tok)
    pieces = []
    for half in halves:
        moved = lax.all_to_all(half, ("gx", "gz"), split_axis=0, concat_axis=0, tiled=True)
        pieces.append(moved.transpose(1, 0, 2).reshape(tok // 2, heads * HEAD_SIZE))
    return jnp.concatenate(pieces, axis=0).reshape(1, tok, heads * HEAD_SIZE)


def solution(mesh):
    nsec, nseq = mesh.devices.shape
    kv_groups = nseq // GROUP
    grid_mesh = Mesh(mesh.devices.reshape(nsec, kv_groups, GROUP), ("section", "gx", "gz"))
    seq = ("gx", "gz")
    return jax.shard_map(
        per_device,
        mesh=grid_mesh,
        in_specs=(
            P("section", seq, None),
            P("section", seq, None),
            P("section", seq, None),
            P("section", seq, None, None),
            P("section", seq, None, None),
            P("section", seq, None),
            P("section", seq),
            P("section", seq, None),
        ),
        out_specs=P("section", seq, None),
        check_vma=False,
    )
```
